512 devices in a mesh: dp: 4 (over x), seq: 8 (over z_lo), tensor: 16 (over z_hi, y, core).
Axes of the slice: x: 4, y: 4, z: 16 (z_hi: 2, z_lo: 8; z = z_hi * 8 + z_lo), core: 2. Of those that a mesh axis runs over, the one named last changes fastest.
Arguments:
- features: bfloat16 [4096, 4096], P(('dp', 'seq'), 'tensor'), parts along dimension 0, may hold values from -6 to 6
- in_weight: bfloat16 [4096, 3, 4096], P('seq', None, 'tensor'), may hold values from -0.09375 to 0.09375
- short_taps: float32 [3, 7, 4096], P(None, None, 'tensor'), may hold values from -2.5 to 2.5
- decay_rates: float32 [16, 4096], P(None, 'tensor'), may hold values from 0.00048828125 to 0.1
- residues: float32 [16, 4096], P(None, 'tensor'), may hold values from -1.5 to 1.5
- skip_gain: float32 [4096], P('tensor'), may hold values from 0.5 to 1.5
- out_weight: bfloat16 [4096, 4096], P(None, 'tensor'), may hold values from -0.09375 to 0.09375
Outputs:
- mixed: bfloat16 [4096, 4096], P(('dp', 'seq'), 'tensor'), parts along dimension 0
The draws below stay inside these ranges and needn't reach their ends.
There are 4 independent parts, one for each index of `dp`. The reference program is written for one: setup_inputs(seed, part) draws one part's arguments, and reference() takes and returns one part's arrays. A program takes and returns all parts, laid end to end along the dimension named above; an argument that names none is the same for every part. Nothing has to cross between parts.
All inputs are finite; a program needn't handle non-finite values.
Results may differ from the reference program's by a relative error of at most 0.007.
Values may be sent and summed in bfloat16 or wider, within the bound.
No kernel may reach another device: no remote copies, remote signals or barrier semaphores. Data moves between devices by JAX's collectives and lax.ppermute only.
A program may use at most 64 MiB of HBM per device.

```python
import math
import jax
import jax.numpy as jnp

D = 4096
KS = 7
M = 16
L = 1024


def block_levels(own_key, shape, split, smallest, top_value):
    def one(dim, blocks):
        steps = jax.random.uniform(jax.random.fold_in(jax.random.fold_in(own_key, 6), dim), (blocks,), jnp.float32, smallest / len(split), top_value / len(split))
        return jnp.repeat(jnp.exp(steps), shape[dim] // blocks).reshape((-1,) + (1,) * (len(shape) - dim - 1))

    loudness = one(*split[0])
    for cut in split[1:]:
        loudness = loudness * one(*cut)
    return loudness


def noise(stream_key, dims, deviation, reach, pieces=(), kind=jnp.bfloat16):
    drawn = jax.random.normal(stream_key, dims, jnp.float32) * deviation
    if len(pieces) > 0:
        drawn = block_levels(stream_key, dims, pieces, -0.22, 0.18) * drawn
    return jnp.clip(drawn, min=-reach, max=reach).astype(kind)


def setup_inputs(seed: int = 0, part: int = 0) -> dict:
    key_of = jax.random.split(jax.random.key(seed), 8)
    own_keys = jax.random.split(jax.random.fold_in(key_of[7], part), 8)
    features = noise(own_keys[0], (L, D), 1.0, 6.0, ((0, 8), (1, 16)))
    in_weight = noise(key_of[1], (D, 3, D), D ** -0.5, 0.09375, ((0, 8), (2, 16)))
    short_taps = noise(key_of[2], (3, KS, D), 0.4, 2.5, ((2, 16),), jnp.float32)
    decay_rates = jnp.clip(jnp.exp(math.log(0.1) - 5.322034 * jax.random.uniform(key_of[3], (M, D), jnp.float32) ** block_levels(key_of[3], (M, D), ((1, 16),), -0.2, 0.2)), 0.00048828125, 0.1)
    residues = noise(key_of[4], (M, D), M ** -0.5, 1.5, ((1, 16),), jnp.float32)
    skip_gain = jnp.clip(0.5 + 1.0 * jax.random.uniform(key_of[5], (D,), jnp.float32) ** block_levels(key_of[5], (D,), ((0, 16),), -0.2, 0.2), 0.5, 1.5)
    out_weight = noise(key_of[6], (D, D), D ** -0.5, 0.09375, ((1, 16),))
    return {"features": features, "in_weight": in_weight, "short_taps": short_taps, "decay_rates": decay_rates, "residues": residues, "skip_gain": skip_gain, "out_weight": out_weight}


def reference(features, in_weight, short_taps, decay_rates, residues, skip_gain, out_weight):
    length = features.shape[0]
    width = features.shape[1]
    projected = jnp.dot(features, in_weight.reshape(width, 3 * width), preferred_element_type=jnp.float32)
    projected = projected.astype(jnp.bfloat16).reshape(length, 3, width)
    taps_count = short_taps.shape[1]
    rim_rows = taps_count - 1
    extended = jnp.concatenate([jnp.zeros((rim_rows, 3, width), jnp.bfloat16), projected], axis=0).astype(jnp.float32)
    short = jnp.zeros((length, 3, width), jnp.float32)
    for offset_lag in range(taps_count):
        short = short + short_taps[:, offset_lag, :][None] * extended[rim_rows - offset_lag:rim_rows - offset_lag + length]
    product = short[:, 1, :] * short[:, 2, :]
    amplitude = residues * jnp.sqrt(2.0 * decay_rates)
    moments = jnp.arange(length).astype(jnp.float32)
    kernel = jnp.zeros((length, width), jnp.float32)
    for mode_index in range(decay_rates.shape[0]):
        kernel = kernel + amplitude[mode_index][None, :] * jnp.exp(-decay_rates[mode_index][None, :] * moments[:, None])
    padded_len = 2 * length
    spectrum = jnp.fft.rfft(product, padded_len, axis=0) * jnp.fft.rfft(kernel, padded_len, axis=0)
    conv = jnp.fft.irfft(spectrum, padded_len, axis=0)[:length]
    gated = (short[:, 0, :] * (conv + skip_gain[None, :] * product)).astype(jnp.bfloat16)
    return jnp.dot(gated, out_weight, preferred_element_type=jnp.float32).astype(jnp.bfloat16)
```

```python
import jax
import jax.numpy as jnp
from jax import lax
from jax.sharding import PartitionSpec as P

precise = lax.Precision.HIGHEST
block_len = 64


def passed_along(value, axis, steps):
    count = lax.axis_size(axis)
    leading, last = (max(0, -steps), min(count, count - steps))
    return lax.ppermute(value, axis, [(source, source + steps) for source in range(leading, last)])


def body(features, in_weight, short_taps, decay_rates, residues, skip_gain, out_weight):
    tok_rows = features.shape[0]
    channels = in_weight.shape[2]
    taps_count = short_taps.shape[1]
    whole_feats = lax.all_gather(features, "tensor", axis=1, tiled=True)
    piece = lax.all_gather(in_weight, "seq", axis=0, tiled=True)
    count = piece.shape[0]
    projected = jnp.dot(
        whole_feats, piece.reshape(count, 3 * channels), preferred_element_type=jnp.float32
    )
    projected = projected.astype(jnp.bfloat16).reshape(tok_rows, 3, channels)
    rim_rows = taps_count - 1
    earlier = passed_along(projected[tok_rows - rim_rows :], "seq", 1)
    extended = jnp.concatenate([earlier, projected], axis=0).astype(jnp.float32)
    short = jnp.zeros((tok_rows, 3, channels), jnp.float32)
    for offset_lag in range(taps_count):
        short = (
            short
            + short_taps[:, offset_lag, :][None]
            * extended[rim_rows - offset_lag : rim_rows - offset_lag + tok_rows]
        )
    product = short[:, 1, :] * short[:, 2, :]
    blocks = tok_rows // block_len
    pieces = product.reshape(blocks, block_len, channels)
    amplitude = residues * jnp.sqrt(2.0 * decay_rates)
    offsets = jnp.arange(block_len).astype(jnp.float32)
    falloff = jnp.exp(-decay_rates[:, None, :] * offsets[None, :, None])
    kernel = jnp.einsum("mc,mtc->tc", amplitude, falloff, precision=precise)
    lag_grid = jnp.arange(block_len)[:, None] - jnp.arange(block_len)[None, :]
    select = (lag_grid[:, :, None] == jnp.arange(block_len)[None, None, :]).astype(jnp.float32)
    toeplitz = jnp.einsum("tsk,kc->tsc", select, kernel, precision=precise)
    inner = jnp.einsum("tsc,bsc->btc", toeplitz, pieces, precision=precise)
    toward_end = jnp.exp(-decay_rates[:, None, :] * (block_len - offsets)[None, :, None])
    block_sums = jnp.einsum("msc,bsc->bmc", toward_end, pieces, precision=precise)
    block_index = jnp.arange(blocks).astype(jnp.float32)
    carry_over = jnp.exp(
        -decay_rates[None] * (block_len * (blocks - 1 - block_index))[:, None, None]
    )
    device_sum = jnp.sum(carry_over * block_sums, axis=0)
    place = lax.axis_index("seq")
    gathered_sums = lax.all_gather(device_sum, "seq")
    earlier_count = jnp.arange(gathered_sums.shape[0])
    distance = (place - 1 - earlier_count).astype(jnp.float32)
    weight = jnp.where(
        (earlier_count < place)[:, None, None],
        jnp.exp(-decay_rates[None] * (float(tok_rows) * jnp.maximum(distance, 0.0))[:, None, None]),
        0.0,
    )
    entering = jnp.sum(weight * gathered_sums, axis=0)
    step_decay = jnp.exp(-decay_rates * float(block_len))

    def advance(state, block_sum):
        return (step_decay * state + block_sum, state)

    final_state, starts = lax.scan(advance, entering, block_sums)
    outer = jnp.einsum("mic,bmc->bic", amplitude[:, None, :] * falloff, starts, precision=precise)
    conv = (inner + outer).reshape(tok_rows, channels)
    gated = (short[:, 0, :] * (conv + skip_gain[None, :] * product)).astype(jnp.bfloat16)
    mixed = jnp.dot(
        lax.all_gather(gated, "tensor", axis=1, tiled=True),
        out_weight,
        preferred_element_type=jnp.float32,
    )
    return mixed.astype(jnp.bfloat16)


def solution(mesh):
    in_specs = (
        P(("dp", "seq"), "tensor"),
        P("seq", None, "tensor"),
        P(None, None, "tensor"),
        P(None, "tensor"),
        P(None, "tensor"),
        P("tensor"),
        P(None, "tensor"),
    )
    out_specs = P(("dp", "seq"), "tensor")
    return jax.shard_map(body, mesh=mesh, in_specs=in_specs, out_specs=out_specs, check_vma=False)
```

```python
import jax
import jax.numpy as jnp
from jax import lax
from jax.sharding import PartitionSpec as P

precise = lax.Precision.HIGHEST
block_len = 64


def gather_weight_rows(features, seq_n, ten_n, halves):
    rounds = []
    for j in range(seq_n * halves):
        i, h = j % seq_n, j // seq_n
        perm = []
        for s in range(seq_n):
            for a in range(seq_n):
                for b in range(halves):
                    src = ((a + i) % seq_n) * ten_n + s * halves + (b + h) % halves
                    perm.append((src, s * ten_n + a * halves + b))
        rounds.append(lax.ppermute(features, ("seq", "tensor"), perm))
    columns = [
        jnp.concatenate(rounds[h * seq_n : (h + 1) * seq_n], axis=0) for h in range(halves)
    ]
    return jnp.concatenate(columns, axis=1)


def body(features, in_weight, short_taps, decay_rates, residues, skip_gain, out_weight):
    seq_n = lax.axis_size("seq")
    ten_n = lax.axis_size("tensor")
    place = lax.axis_index("seq")
    lane = lax.axis_index("tensor")
    tok_rows, fcols = features.shape
    rows_here, branches, channels = in_weight.shape
    halves = rows_here // fcols
    sub = channels // seq_n
    length = tok_rows * seq_n
    taps_count = short_taps.shape[1]
    rotation = lane // halves
    half_of = lane % halves

    rows_of_feats = gather_weight_rows(features, seq_n, ten_n, halves)
    doubled = jnp.concatenate([in_weight, in_weight], axis=0)
    weight_rows = lax.dynamic_slice_in_dim(doubled, half_of * fcols, rows_here, axis=0)
    weight_rows = weight_rows.reshape(rows_here, branches, seq_n, sub)
    partial = jnp.einsum(
        "td,djgc->gtjc", rows_of_feats, weight_rows, preferred_element_type=jnp.float32
    )
    summed = lax.psum_scatter(partial.reshape(seq_n * length, -1), "seq", scatter_dimension=0, tiled=True)
    summed = jnp.roll(summed.reshape(length, branches, sub), rotation * tok_rows, axis=0)
    projected = lax.reduce_precision(summed, exponent_bits=8, mantissa_bits=7)

    taps = lax.dynamic_slice_in_dim(short_taps, place * sub, sub, axis=2)
    decay = lax.dynamic_slice_in_dim(decay_rates, place * sub, sub, axis=1)
    resid = lax.dynamic_slice_in_dim(residues, place * sub, sub, axis=1)
    skip = lax.dynamic_slice_in_dim(skip_gain, place * sub, sub, axis=0)

    rim_rows = taps_count - 1
    extended = jnp.concatenate(
        [jnp.zeros((rim_rows, branches, sub), jnp.float32), projected], axis=0
    )
    short = jnp.zeros((length, branches, sub), jnp.float32)
    for offset_lag in range(taps_count):
        short = (
            short
            + taps[:, offset_lag, :][None]
            * extended[rim_rows - offset_lag : rim_rows - offset_lag + length]
        )
    product = short[:, 1, :] * short[:, 2, :]
    blocks = length // block_len
    pieces = product.reshape(blocks, block_len, sub)
    amplitude = resid * jnp.sqrt(2.0 * decay)
    offsets = jnp.arange(block_len).astype(jnp.float32)
    falloff = jnp.exp(-decay[:, None, :] * offsets[None, :, None])
    kernel = jnp.einsum("mc,mtc->tc", amplitude, falloff, precision=precise)
    lag_grid = jnp.arange(block_len)[:, None] - jnp.arange(block_len)[None, :]
    select = (lag_grid[:, :, None] == jnp.arange(block_len)[None, None, :]).astype(jnp.float32)
    toeplitz = jnp.einsum("tsk,kc->tsc", select, kernel, precision=precise)
    inner = jnp.einsum("tsc,bsc->btc", toeplitz, pieces, precision=precise)
    toward_end = jnp.exp(-decay[:, None, :] * (block_len - offsets)[None, :, None])
    block_sums = jnp.einsum("msc,bsc->bmc", toward_end, pieces, precision=precise)
    later = jnp.arange(blocks)[:, None]
    earlier = jnp.arange(blocks)[None, :]
    distance = jnp.maximum(later - 1 - earlier, 0).astype(jnp.float32)
    carry = jnp.where(
        (earlier < later)[:, :, None, None],
        jnp.exp(-decay[None, None] * (block_len * distance)[:, :, None, None]),
        0.0,
    )
    starts = jnp.sum(carry * block_sums[None], axis=1)
    outer = jnp.einsum("mic,bmc->bic", amplitude[:, None, :] * falloff, starts, precision=precise)
    conv = (inner + outer).reshape(length, sub)
    gated = (short[:, 0, :] * (conv + skip[None, :] * product)).astype(jnp.bfloat16)
    gated = lax.all_to_all(gated, "seq", 0, 1, tiled=True)
    mixed = jnp.dot(
        lax.all_gather(gated, "tensor", axis=1, tiled=True),
        out_weight,
        preferred_element_type=jnp.float32,
    )
    return mixed.astype(jnp.bfloat16)


def solution(mesh):
    in_specs = (
        P(("dp", "seq"), "tensor"),
        P("seq", None, "tensor"),
        P(None, None, "tensor"),
        P(None, "tensor"),
        P(None, "tensor"),
        P("tensor"),
        P(None, "tensor"),
    )
    out_specs = P(("dp", "seq"), "tensor")
    return jax.shard_map(body, mesh=mesh, in_specs=in_specs, out_specs=out_specs, check_vma=False)
```

```python
import jax
import jax.numpy as jnp
from jax import lax
from jax.sharding import PartitionSpec as P

precise = lax.Precision.HIGHEST
block_len = 64


def body(features, in_weight, short_taps, decay_rates, residues, skip_gain, out_weight):
    seq_n = lax.axis_size("seq")
    ten_n = lax.axis_size("tensor")
    place = lax.axis_index("seq")
    lane = lax.axis_index("tensor")
    tok_rows, fcols = features.shape
    rows_here, branches, channels = in_weight.shape
    halves = rows_here // fcols
    sub = channels // seq_n
    length = tok_rows * seq_n
    taps_count = short_taps.shape[1]
    copies = jnp.tile(features, (ten_n, 1))
    own_tokens = lax.all_to_all(copies, "tensor", 0, 1, tiled=True)
    rows_of_feats = lax.all_to_all(own_tokens, "seq", 1, 0, tiled=True)
    weight_rows = in_weight.reshape(rows_here, branches, seq_n, sub)
    partial = jnp.einsum(
        "td,djgc->gtjc", rows_of_feats, weight_rows, preferred_element_type=jnp.float32
    )
    summed = lax.psum_scatter(partial.reshape(seq_n * length, -1), "seq", scatter_dimension=0, tiled=True)
    summed = summed.reshape(length, branches, sub)
    projected = lax.reduce_precision(summed, exponent_bits=8, mantissa_bits=7)

    taps = lax.dynamic_slice_in_dim(short_taps, place * sub, sub, axis=2)
    decay = lax.dynamic_slice_in_dim(decay_rates, place * sub, sub, axis=1)
    resid = lax.dynamic_slice_in_dim(residues, place * sub, sub, axis=1)
    skip = lax.dynamic_slice_in_dim(skip_gain, place * sub, sub, axis=0)

    rim_rows = taps_count - 1
    extended = jnp.concatenate(
        [jnp.zeros((rim_rows, branches, sub), jnp.float32), projected], axis=0
    )
    short = jnp.zeros((length, branches, sub), jnp.float32)
    for offset_lag in range(taps_count):
        short = (
            short
            + taps[:, offset_lag, :][None]
            * extended[rim_rows - offset_lag : rim_rows - offset_lag + length]
        )
    product = short[:, 1, :] * short[:, 2, :]
    blocks = length // block_len
    pieces = product.reshape(blocks, block_len, sub)
    amplitude = resid * jnp.sqrt(2.0 * decay)
    offsets = jnp.arange(block_len).astype(jnp.float32)
    falloff = jnp.exp(-decay[:, None, :] * offsets[None, :, None])
    kernel = jnp.einsum("mc,mtc->tc", amplitude, falloff, precision=precise)
    lag_grid = jnp.arange(block_len)[:, None] - jnp.arange(block_len)[None, :]
    select = (lag_grid[:, :, None] == jnp.arange(block_len)[None, None, :]).astype(jnp.float32)
    toeplitz = jnp.einsum("tsk,kc->tsc", select, kernel, precision=precise)
    inner = jnp.einsum("tsc,bsc->btc", toeplitz, pieces, precision=precise)
    toward_end = jnp.exp(-decay[:, None, :] * (block_len - offsets)[None, :, None])
    block_sums = jnp.einsum("msc,bsc->bmc", toward_end, pieces, precision=precise)
    later = jnp.arange(blocks)[:, None]
    earlier = jnp.arange(blocks)[None, :]
    distance = jnp.maximum(later - 1 - earlier, 0).astype(jnp.float32)
    carry = jnp.where(
        (earlier < later)[:, :, None, None],
        jnp.exp(-decay[None, None] * (block_len * distance)[:, :, None, None]),
        0.0,
    )
    starts = jnp.sum(carry * block_sums[None], axis=1)
    outer = jnp.einsum("mic,bmc->bic", amplitude[:, None, :] * falloff, starts, precision=precise)
    conv = (inner + outer).reshape(length, sub)
    gated = (short[:, 0, :] * (conv + skip[None, :] * product)).astype(jnp.bfloat16)
    outgoing = jnp.broadcast_to(
        gated.reshape(seq_n, 1, tok_rows, sub), (seq_n, ten_n, tok_rows, sub)
    ).reshape(seq_n * ten_n * tok_rows, sub)
    incoming = lax.all_to_all(outgoing, ("seq", "tensor"), 0, 0, tiled=True)
    incoming = incoming.reshape(seq_n, ten_n, tok_rows, sub).transpose(2, 1, 0, 3)
    mixed = jnp.dot(
        incoming.reshape(tok_rows, ten_n * seq_n * sub),
        out_weight,
        preferred_element_type=jnp.float32,
    )
    return mixed.astype(jnp.bfloat16)


def solution(mesh):
    in_specs = (
        P(("dp", "seq"), "tensor"),
        P("seq", None, "tensor"),
        P(None, None, "tensor"),
        P(None, "tensor"),
        P(None, "tensor"),
        P("tensor"),
        P(None, "tensor"),
    )
    out_specs = P(("dp", "seq"), "tensor")
    return jax.shard_map(body, mesh=mesh, in_specs=in_specs, out_specs=out_specs, check_vma=False)
```

```python
import jax
import jax.numpy as jnp
from jax import lax
from jax.sharding import PartitionSpec as P

precise = lax.Precision.HIGHEST
block_len = 64


def body(features, in_weight, short_taps, decay_rates, residues, skip_gain, out_weight):
    seq_n = lax.axis_size("seq")
    ten_n = lax.axis_size("tensor")
    place = lax.axis_index("seq")
    lane = lax.axis_index("tensor")
    tok_rows, fcols = features.shape
    rows_here, branches, channels = in_weight.shape
    halves = rows_here // fcols
    sub = channels // seq_n
    length = tok_rows * seq_n
    taps_count = short_taps.shape[1]
    copies = jnp.tile(features, (seq_n, 1))
    my_columns = lax.all_to_all(copies, "seq", 0, 0, tiled=True)
    across = []
    for s in range(seq_n):
        for a in range(seq_n):
            for b in range(halves):
                across.append((a * ten_n + s * halves + b, s * ten_n + a * halves + b))
    first = lax.ppermute(my_columns, ("seq", "tensor"), across)
    swap = [(k, k + 1 - 2 * (k % 2)) for k in range(ten_n)]
    second = lax.ppermute(first, "tensor", swap)
    rows_of_feats = jnp.concatenate([first, second], axis=1)
    half_of = lane % halves
    doubled = jnp.concatenate([in_weight, in_weight], axis=0)
    weight_rows = lax.dynamic_slice_in_dim(doubled, half_of * fcols, rows_here, axis=0)
    weight_rows = weight_rows.reshape(rows_here, branches, seq_n, sub)
    partial = jnp.einsum(
        "td,djgc->gtjc", rows_of_feats, weight_rows, preferred_element_type=jnp.float32
    )
    summed = lax.psum_scatter(partial.reshape(seq_n * length, -1), "seq", scatter_dimension=0, tiled=True)
    summed = summed.reshape(length, branches, sub)
    projected = lax.reduce_precision(summed, exponent_bits=8, mantissa_bits=7)

    taps = lax.dynamic_slice_in_dim(short_taps, place * sub, sub, axis=2)
    decay = lax.dynamic_slice_in_dim(decay_rates, place * sub, sub, axis=1)
    resid = lax.dynamic_slice_in_dim(residues, place * sub, sub, axis=1)
    skip = lax.dynamic_slice_in_dim(skip_gain, place * sub, sub, axis=0)

    rim_rows = taps_count - 1
    extended = jnp.concatenate(
        [jnp.zeros((rim_rows, branches, sub), jnp.float32), projected], axis=0
    )
    short = jnp.zeros((length, branches, sub), jnp.float32)
    for offset_lag in range(taps_count):
        short = (
            short
            + taps[:, offset_lag, :][None]
            * extended[rim_rows - offset_lag : rim_rows - offset_lag + length]
        )
    product = short[:, 1, :] * short[:, 2, :]
    blocks = length // block_len
    pieces = product.reshape(blocks, block_len, sub)
    amplitude = resid * jnp.sqrt(2.0 * decay)
    offsets = jnp.arange(block_len).astype(jnp.float32)
    falloff = jnp.exp(-decay[:, None, :] * offsets[None, :, None])
    kernel = jnp.einsum("mc,mtc->tc", amplitude, falloff, precision=precise)
    lag_grid = jnp.arange(block_len)[:, None] - jnp.arange(block_len)[None, :]
    select = (lag_grid[:, :, None] == jnp.arange(block_len)[None, None, :]).astype(jnp.float32)
    toeplitz = jnp.einsum("tsk,kc->tsc", select, kernel, precision=precise)
    inner = jnp.einsum("tsc,bsc->btc", toeplitz, pieces, precision=precise)
    toward_end = jnp.exp(-decay[:, None, :] * (block_len - offsets)[None, :, None])
    block_sums = jnp.einsum("msc,bsc->bmc", toward_end, pieces, precision=precise)
    later = jnp.arange(blocks)[:, None]
    earlier = jnp.arange(blocks)[None, :]
    distance = jnp.maximum(later - 1 - earlier, 0).astype(jnp.float32)
    carry = jnp.where(
        (earlier < later)[:, :, None, None],
        jnp.exp(-decay[None, None] * (block_len * distance)[:, :, None, None]),
        0.0,
    )
    starts = jnp.sum(carry * block_sums[None], axis=1)
    outer = jnp.einsum("mic,bmc->bic", amplitude[:, None, :] * falloff, starts, precision=precise)
    conv = (inner + outer).reshape(length, sub)
    gated = (short[:, 0, :] * (conv + skip[None, :] * product)).astype(jnp.bfloat16)
    outgoing = jnp.broadcast_to(
        gated.reshape(seq_n, 1, tok_rows, sub), (seq_n, ten_n, tok_rows, sub)
    ).reshape(seq_n * ten_n * tok_rows, sub)
    incoming = lax.all_to_all(outgoing, ("seq", "tensor"), 0, 0, tiled=True)
    incoming = incoming.reshape(seq_n, ten_n, tok_rows, sub).transpose(2, 1, 0, 3)
    mixed = jnp.dot(
        incoming.reshape(tok_rows, ten_n * seq_n * sub),
        out_weight,
        preferred_element_type=jnp.float32,
    )
    return mixed.astype(jnp.bfloat16)


def solution(mesh):
    in_specs = (
        P(("dp", "seq"), "tensor"),
        P("seq", None, "tensor"),
        P(None, None, "tensor"),
        P(None, "tensor"),
        P(None, "tensor"),
        P("tensor"),
        P(None, "tensor"),
    )
    out_specs = P(("dp", "seq"), "tensor")
    return jax.shard_map(body, mesh=mesh, in_specs=in_specs, out_specs=out_specs, check_vma=False)
```

```python
import jax
import jax.numpy as jnp
from jax import lax
from jax.sharding import PartitionSpec as P

precise = lax.Precision.HIGHEST
block_len = 64


def mix_channels(projected, taps, decay, resid, skip):
    length, branches, sub = projected.shape
    taps_count = taps.shape[1]

    rim_rows = taps_count - 1
    extended = jnp.concatenate(
        [jnp.zeros((rim_rows, branches, sub), jnp.float32), projected], axis=0
    )
    short = jnp.zeros((length, branches, sub), jnp.float32)
    for offset_lag in range(taps_count):
        short = (
            short
            + taps[:, offset_lag, :][None]
            * extended[rim_rows - offset_lag : rim_rows - offset_lag + length]
        )
    product = short[:, 1, :] * short[:, 2, :]
    blocks = length // block_len
    pieces = product.reshape(blocks, block_len, sub)
    amplitude = resid * jnp.sqrt(2.0 * decay)
    offsets = jnp.arange(block_len).astype(jnp.float32)
    falloff = jnp.exp(-decay[:, None, :] * offsets[None, :, None])
    kernel = jnp.einsum("mc,mtc->tc", amplitude, falloff, precision=precise)
    lag_grid = jnp.arange(block_len)[:, None] - jnp.arange(block_len)[None, :]
    select = (lag_grid[:, :, None] == jnp.arange(block_len)[None, None, :]).astype(jnp.float32)
    toeplitz = jnp.einsum("tsk,kc->tsc", select, kernel, precision=precise)
    inner = jnp.einsum("tsc,bsc->btc", toeplitz, pieces, precision=precise)
    toward_end = jnp.exp(-decay[:, None, :] * (block_len - offsets)[None, :, None])
    block_sums = jnp.einsum("msc,bsc->bmc", toward_end, pieces, precision=precise)
    later = jnp.arange(blocks)[:, None]
    earlier = jnp.arange(blocks)[None, :]
    distance = jnp.maximum(later - 1 - earlier, 0).astype(jnp.float32)
    carry = jnp.where(
        (earlier < later)[:, :, None, None],
        jnp.exp(-decay[None, None] * (block_len * distance)[:, :, None, None]),
        0.0,
    )
    starts = jnp.sum(carry * block_sums[None], axis=1)
    outer = jnp.einsum("mic,bmc->bic", amplitude[:, None, :] * falloff, starts, precision=precise)
    conv = (inner + outer).reshape(length, sub)
    gated = (short[:, 0, :] * (conv + skip[None, :] * product)).astype(jnp.bfloat16)
    return gated


def body(features, in_weight, short_taps, decay_rates, residues, skip_gain, out_weight):
    seq_n = lax.axis_size("seq")
    ten_n = lax.axis_size("tensor")
    place = lax.axis_index("seq")
    lane = lax.axis_index("tensor")
    tok_rows, fcols = features.shape
    rows_here, branches, channels = in_weight.shape
    halves = rows_here // fcols
    sub = channels // seq_n
    length = tok_rows * seq_n
    chunks = 2
    copies = jnp.tile(features, (seq_n, 1))
    my_columns = lax.all_to_all(copies, "seq", 0, 0, tiled=True)
    across = []
    for s in range(seq_n):
        for a in range(seq_n):
            for b in range(halves):
                across.append((a * ten_n + s * halves + b, s * ten_n + a * halves + b))
    first = lax.ppermute(my_columns, ("seq", "tensor"), across)
    swap = [(k, k + 1 - 2 * (k % 2)) for k in range(ten_n)]
    second = lax.ppermute(first, "tensor", swap)
    rows_of_feats = jnp.concatenate([first, second], axis=1)
    half_of = lane % halves
    doubled = jnp.concatenate([in_weight, in_weight], axis=0)
    weight_rows = lax.dynamic_slice_in_dim(doubled, half_of * fcols, rows_here, axis=0)
    weight_rows = weight_rows.reshape(rows_here, branches, seq_n, sub)
    partial = jnp.einsum(
        "td,djgc->gtjc", rows_of_feats, weight_rows, preferred_element_type=jnp.float32
    )
    taps = lax.dynamic_slice_in_dim(short_taps, place * sub, sub, axis=2)
    decay = lax.dynamic_slice_in_dim(decay_rates, place * sub, sub, axis=1)
    resid = lax.dynamic_slice_in_dim(residues, place * sub, sub, axis=1)
    skip = lax.dynamic_slice_in_dim(skip_gain, place * sub, sub, axis=0)
    weight_out = out_weight.reshape(ten_n, seq_n, chunks, sub // chunks, -1)
    part_len = sub // chunks
    mixed = None
    for q in range(chunks):
        cut = slice(q * part_len, (q + 1) * part_len)
        piece = partial[..., cut].reshape(seq_n * length, branches * part_len)
        summed = lax.psum_scatter(piece, "seq", scatter_dimension=0, tiled=True)
        projected = lax.reduce_precision(
            summed.reshape(length, branches, part_len), exponent_bits=8, mantissa_bits=7
        )
        gated = mix_channels(projected, taps[..., cut], decay[:, cut], resid[:, cut], skip[cut])
        outgoing = jnp.broadcast_to(
            gated.reshape(seq_n, 1, tok_rows, part_len), (seq_n, ten_n, tok_rows, part_len)
        ).reshape(seq_n * ten_n * tok_rows, part_len)
        incoming = lax.all_to_all(outgoing, ("seq", "tensor"), 0, 0, tiled=True)
        incoming = incoming.reshape(seq_n, ten_n, tok_rows, part_len).transpose(2, 1, 0, 3)
        rows = weight_out[:, :, q].reshape(ten_n * seq_n * part_len, -1)
        term = jnp.dot(
            incoming.reshape(tok_rows, ten_n * seq_n * part_len),
            rows,
            preferred_element_type=jnp.float32,
        )
        mixed = term if mixed is None else mixed + term
    return mixed.astype(jnp.bfloat16)


def solution(mesh):
    in_specs = (
        P(("dp", "seq"), "tensor"),
        P("seq", None, "tensor"),
        P(None, None, "tensor"),
        P(None, "tensor"),
        P(None, "tensor"),
        P("tensor"),
        P(None, "tensor"),
    )
    out_specs = P(("dp", "seq"), "tensor")
    return jax.shard_map(body, mesh=mesh, in_specs=in_specs, out_specs=out_specs, check_vma=False)
```

```python
import jax
import jax.numpy as jnp
from jax import lax
from jax.sharding import PartitionSpec as P

precise = lax.Precision.HIGHEST
block_len = 64


def body(features, in_weight, short_taps, decay_rates, residues, skip_gain, out_weight):
    seq_n = lax.axis_size("seq")
    outer_n = lax.axis_size("zhi")
    inner_n = lax.axis_size("inner")
    ten_n = outer_n * inner_n
    place = lax.axis_index("seq")
    far = lax.axis_index("zhi")
    lane = far * inner_n + lax.axis_index("inner")
    tok_rows, fcols = features.shape
    rows_here, branches, channels = in_weight.shape
    halves = rows_here // fcols
    sub = channels // seq_n
    length = tok_rows * seq_n
    taps_count = short_taps.shape[1]
    copies = jnp.tile(features, (seq_n, 1))
    my_columns = lax.all_to_all(copies, "seq", 0, 0, tiled=True)
    across = []
    for s in range(seq_n):
        for a in range(seq_n):
            for b in range(halves):
                across.append((a * ten_n + s * halves + b, s * ten_n + a * halves + b))
    first = lax.ppermute(my_columns, ("seq", "zhi", "inner"), across)
    swap = [(k, k + 1 - 2 * (k % 2)) for k in range(inner_n)]
    second = lax.ppermute(first, "inner", swap)
    rows_of_feats = jnp.concatenate([first, second], axis=1)
    half_of = lane % halves
    doubled = jnp.concatenate([in_weight, in_weight], axis=0)
    weight_rows = lax.dynamic_slice_in_dim(doubled, half_of * fcols, rows_here, axis=0)
    weight_rows = weight_rows.reshape(rows_here, branches, seq_n, sub)
    partial = jnp.einsum(
        "td,djgc->gtjc", rows_of_feats, weight_rows, preferred_element_type=jnp.float32
    )
    summed = lax.psum_scatter(partial.reshape(seq_n * length, -1), "seq", scatter_dimension=0, tiled=True)
    summed = summed.reshape(length, branches, sub)
    projected = lax.reduce_precision(summed, exponent_bits=8, mantissa_bits=7)

    taps = lax.dynamic_slice_in_dim(short_taps, place * sub, sub, axis=2)
    decay = lax.dynamic_slice_in_dim(decay_rates, place * sub, sub, axis=1)
    resid = lax.dynamic_slice_in_dim(residues, place * sub, sub, axis=1)
    skip = lax.dynamic_slice_in_dim(skip_gain, place * sub, sub, axis=0)

    rim_rows = taps_count - 1
    extended = jnp.concatenate(
        [jnp.zeros((rim_rows, branches, sub), jnp.float32), projected], axis=0
    )
    short = jnp.zeros((length, branches, sub), jnp.float32)
    for offset_lag in range(taps_count):
        short = (
            short
            + taps[:, offset_lag, :][None]
            * extended[rim_rows - offset_lag : rim_rows - offset_lag + length]
        )
    product = short[:, 1, :] * short[:, 2, :]
    blocks = length // block_len
    pieces = product.reshape(blocks, block_len, sub)
    amplitude = resid * jnp.sqrt(2.0 * decay)
    offsets = jnp.arange(block_len).astype(jnp.float32)
    falloff = jnp.exp(-decay[:, None, :] * offsets[None, :, None])
    kernel = jnp.einsum("mc,mtc->tc", amplitude, falloff, precision=precise)
    lag_grid = jnp.arange(block_len)[:, None] - jnp.arange(block_len)[None, :]
    select = (lag_grid[:, :, None] == jnp.arange(block_len)[None, None, :]).astype(jnp.float32)
    toeplitz = jnp.einsum("tsk,kc->tsc", select, kernel, precision=precise)
    inner = jnp.einsum("tsc,bsc->btc", toeplitz, pieces, precision=precise)
    toward_end = jnp.exp(-decay[:, None, :] * (block_len - offsets)[None, :, None])
    block_sums = jnp.einsum("msc,bsc->bmc", toward_end, pieces, precision=precise)
    later = jnp.arange(blocks)[:, None]
    earlier = jnp.arange(blocks)[None, :]
    distance = jnp.maximum(later - 1 - earlier, 0).astype(jnp.float32)
    carry = jnp.where(
        (earlier < later)[:, :, None, None],
        jnp.exp(-decay[None, None] * (block_len * distance)[:, :, None, None]),
        0.0,
    )
    starts = jnp.sum(carry * block_sums[None], axis=1)
    outer = jnp.einsum("mic,bmc->bic", amplitude[:, None, :] * falloff, starts, precision=precise)
    conv = (inner + outer).reshape(length, sub)
    gated = (short[:, 0, :] * (conv + skip[None, :] * product)).astype(jnp.bfloat16)
    gated = lax.all_to_all(gated, "seq", 0, 1, tiled=True)
    opposite = lax.ppermute(gated, "zhi", [(z, outer_n - 1 - z) for z in range(outer_n)])
    pair = jnp.where(far == 0, jnp.stack([gated, opposite], 1), jnp.stack([opposite, gated], 1))
    whole = lax.all_gather(pair, "inner", axis=2, tiled=False)
    mixed = jnp.dot(
        whole.reshape(tok_rows, ten_n * channels),
        out_weight,
        preferred_element_type=jnp.float32,
    )
    return mixed.astype(jnp.bfloat16)


def solution(mesh):
    devices = mesh.devices
    halves_mesh = jax.sharding.Mesh(
        devices.reshape(devices.shape[0], devices.shape[1], 2, devices.shape[2] // 2),
        ("dp", "seq", "zhi", "inner"),
    )
    tensor = ("zhi", "inner")
    in_specs = (
        P(("dp", "seq"), tensor),
        P("seq", None, tensor),
        P(None, None, tensor),
        P(None, tensor),
        P(None, tensor),
        P(tensor),
        P(None, tensor),
    )
    out_specs = P(("dp", "seq"), tensor)
    return jax.shard_map(
        body, mesh=halves_mesh, in_specs=in_specs, out_specs=out_specs, check_vma=False
    )
```

```python
import jax
import jax.numpy as jnp
from jax import lax
from jax.sharding import PartitionSpec as P

precise = lax.Precision.HIGHEST
block_len = 64


def body(features, in_weight, short_taps, decay_rates, residues, skip_gain, out_weight):
    seq_n = lax.axis_size("seq")
    outer_n = lax.axis_size("zhi")
    inner_n = lax.axis_size("inner")
    ten_n = outer_n * inner_n
    place = lax.axis_index("seq")
    far = lax.axis_index("zhi")
    lane = far * inner_n + lax.axis_index("inner")
    tok_rows, fcols = features.shape
    rows_here, branches, channels = in_weight.shape
    halves = rows_here // fcols
    sub = channels // seq_n
    length = tok_rows * seq_n
    taps_count = short_taps.shape[1]
    copies = jnp.tile(features, (seq_n, 1))
    my_columns = lax.all_to_all(copies, "seq", 0, 0, tiled=True)
    y_n = inner_n // halves

    def spot(s, z, y, b):
        return (s * outer_n + z) * inner_n + y * halves + b

    def root_of(s, b):
        k = s * halves + b
        return k // inner_n, (k % inner_n) // halves

    over = []
    for s in range(seq_n):
        for b in range(halves):
            z_r, y_r = root_of(s, b)
            over.append((spot(s, z_r, y_r, b), spot(s, outer_n - 1 - z_r, y_r, b)))
    crossed = lax.ppermute(my_columns, ("seq", "zhi", "inner"), over)
    inner = lax.axis_index("inner")
    my_y = inner // halves
    my_b = inner % halves
    root_k = place * halves + my_b
    root_z = root_k // inner_n
    root_y = (root_k % inner_n) // halves
    relay = jnp.where(far == root_z, my_columns, crossed)
    first = jnp.where(far == root_z, my_columns, crossed)
    shift = (my_y - root_y) % y_n
    for o in range(1, y_n):
        along = []
        for s in range(seq_n):
            for z in range(outer_n):
                for b in range(halves):
                    _, y_r = root_of(s, b)
                    along.append((spot(s, z, y_r, b), spot(s, z, (y_r + o) % y_n, b)))
        moved = lax.ppermute(relay, ("seq", "zhi", "inner"), along)
        first = jnp.where(shift == o, moved, first)
    swap = [(k, k + 1 - 2 * (k % 2)) for k in range(inner_n)]
    second = lax.ppermute(first, "inner", swap)
    rows_of_feats = jnp.concatenate([first, second], axis=1)
    half_of = lane % halves
    doubled = jnp.concatenate([in_weight, in_weight], axis=0)
    weight_rows = lax.dynamic_slice_in_dim(doubled, half_of * fcols, rows_here, axis=0)
    weight_rows = weight_rows.reshape(rows_here, branches, seq_n, sub)
    partial = jnp.einsum(
        "td,djgc->gtjc", rows_of_feats, weight_rows, preferred_element_type=jnp.float32
    )
    summed = lax.psum_scatter(partial.reshape(seq_n * length, -1), "seq", scatter_dimension=0, tiled=True)
    summed = summed.reshape(length, branches, sub)
    projected = lax.reduce_precision(summed, exponent_bits=8, mantissa_bits=7)

    taps = lax.dynamic_slice_in_dim(short_taps, place * sub, sub, axis=2)
    decay = lax.dynamic_slice_in_dim(decay_rates, place * sub, sub, axis=1)
    resid = lax.dynamic_slice_in_dim(residues, place * sub, sub, axis=1)
    skip = lax.dynamic_slice_in_dim(skip_gain, place * sub, sub, axis=0)

    rim_rows = taps_count - 1
    extended = jnp.concatenate(
        [jnp.zeros((rim_rows, branches, sub), jnp.float32), projected], axis=0
    )
    short = jnp.zeros((length, branches, sub), jnp.float32)
    for offset_lag in range(taps_count):
        short = (
            short
            + taps[:, offset_lag, :][None]
            * extended[rim_rows - offset_lag : rim_rows - offset_lag + length]
        )
    product = short[:, 1, :] * short[:, 2, :]
    blocks = length // block_len
    pieces = product.reshape(blocks, block_len, sub)
    amplitude = resid * jnp.sqrt(2.0 * decay)
    offsets = jnp.arange(block_len).astype(jnp.float32)
    falloff = jnp.exp(-decay[:, None, :] * offsets[None, :, None])
    kernel = jnp.einsum("mc,mtc->tc", amplitude, falloff, precision=precise)
    lag_grid = jnp.arange(block_len)[:, None] - jnp.arange(block_len)[None, :]
    select = (lag_grid[:, :, None] == jnp.arange(block_len)[None, None, :]).astype(jnp.float32)
    toeplitz = jnp.einsum("tsk,kc->tsc", select, kernel, precision=precise)
    inner = jnp.einsum("tsc,bsc->btc", toeplitz, pieces, precision=precise)
    toward_end = jnp.exp(-decay[:, None, :] * (block_len - offsets)[None, :, None])
    block_sums = jnp.einsum("msc,bsc->bmc", toward_end, pieces, precision=precise)
    later = jnp.arange(blocks)[:, None]
    earlier = jnp.arange(blocks)[None, :]
    distance = jnp.maximum(later - 1 - earlier, 0).astype(jnp.float32)
    carry = jnp.where(
        (earlier < later)[:, :, None, None],
        jnp.exp(-decay[None, None] * (block_len * distance)[:, :, None, None]),
        0.0,
    )
    starts = jnp.sum(carry * block_sums[None], axis=1)
    outer = jnp.einsum("mic,bmc->bic", amplitude[:, None, :] * falloff, starts, precision=precise)
    conv = (inner + outer).reshape(length, sub)
    gated = (short[:, 0, :] * (conv + skip[None, :] * product)).astype(jnp.bfloat16)
    gated = lax.all_to_all(gated, "seq", 0, 1, tiled=True)
    opposite = lax.ppermute(gated, "zhi", [(z, outer_n - 1 - z) for z in range(outer_n)])
    pair = jnp.where(far == 0, jnp.stack([gated, opposite], 1), jnp.stack([opposite, gated], 1))
    whole = lax.all_gather(pair, "inner", axis=2, tiled=False)
    mixed = jnp.dot(
        whole.reshape(tok_rows, ten_n * channels),
        out_weight,
        preferred_element_type=jnp.float32,
    )
    return mixed.astype(jnp.bfloat16)


def solution(mesh):
    devices = mesh.devices
    halves_mesh = jax.sharding.Mesh(
        devices.reshape(devices.shape[0], devices.shape[1], 2, devices.shape[2] // 2),
        ("dp", "seq", "zhi", "inner"),
    )
    tensor = ("zhi", "inner")
    in_specs = (
        P(("dp", "seq"), tensor),
        P("seq", None, tensor),
        P(None, None, tensor),
        P(None, tensor),
        P(None, tensor),
        P(tensor),
        P(None, tensor),
    )
    out_specs = P(("dp", "seq"), tensor)
    return jax.shard_map(
        body, mesh=halves_mesh, in_specs=in_specs, out_specs=out_specs, check_vma=False
    )
```

```python
import jax
import jax.numpy as jnp
from jax import lax
from jax.sharding import PartitionSpec as P

precise = lax.Precision.HIGHEST
block_len = 64


def body(features, in_weight, short_taps, decay_rates, residues, skip_gain, out_weight):
    seq_n = lax.axis_size("seq")
    outer_n = lax.axis_size("zhi")
    inner_n = lax.axis_size("inner")
    ten_n = outer_n * inner_n
    place = lax.axis_index("seq")
    far = lax.axis_index("zhi")
    lane = far * inner_n + lax.axis_index("inner")
    tok_rows, fcols = features.shape
    rows_here, branches, channels = in_weight.shape
    halves = rows_here // fcols
    sub = channels // seq_n
    length = tok_rows * seq_n
    taps_count = short_taps.shape[1]
    copies = jnp.tile(features, (ten_n, 1))
    own_tokens = lax.all_to_all(copies, ("zhi", "inner"), 0, 1, tiled=True)
    whole_weight = lax.all_gather(in_weight, "seq", axis=0, tiled=True)
    local = jnp.dot(
        own_tokens,
        whole_weight.reshape(seq_n * rows_here, branches * channels),
        preferred_element_type=jnp.float32,
    ).astype(jnp.bfloat16)
    local = local.reshape(tok_rows, branches, seq_n, sub).transpose(2, 0, 1, 3)
    projected = lax.all_to_all(local, "seq", 0, 1, tiled=True)
    projected = projected.reshape(length, branches, sub).astype(jnp.float32)

    taps = lax.dynamic_slice_in_dim(short_taps, place * sub, sub, axis=2)
    decay = lax.dynamic_slice_in_dim(decay_rates, place * sub, sub, axis=1)
    resid = lax.dynamic_slice_in_dim(residues, place * sub, sub, axis=1)
    skip = lax.dynamic_slice_in_dim(skip_gain, place * sub, sub, axis=0)

    rim_rows = taps_count - 1
    extended = jnp.concatenate(
        [jnp.zeros((rim_rows, branches, sub), jnp.float32), projected], axis=0
    )
    short = jnp.zeros((length, branches, sub), jnp.float32)
    for offset_lag in range(taps_count):
        short = (
            short
            + taps[:, offset_lag, :][None]
            * extended[rim_rows - offset_lag : rim_rows - offset_lag + length]
        )
    product = short[:, 1, :] * short[:, 2, :]
    blocks = length // block_len
    pieces = product.reshape(blocks, block_len, sub)
    amplitude = resid * jnp.sqrt(2.0 * decay)
    offsets = jnp.arange(block_len).astype(jnp.float32)
    falloff = jnp.exp(-decay[:, None, :] * offsets[None, :, None])
    kernel = jnp.einsum("mc,mtc->tc", amplitude, falloff, precision=precise)
    lag_grid = jnp.arange(block_len)[:, None] - jnp.arange(block_len)[None, :]
    select = (lag_grid[:, :, None] == jnp.arange(block_len)[None, None, :]).astype(jnp.float32)
    toeplitz = jnp.einsum("tsk,kc->tsc", select, kernel, precision=precise)
    inner = jnp.einsum("tsc,bsc->btc", toeplitz, pieces, precision=precise)
    toward_end = jnp.exp(-decay[:, None, :] * (block_len - offsets)[None, :, None])
    block_sums = jnp.einsum("msc,bsc->bmc", toward_end, pieces, precision=precise)
    later = jnp.arange(blocks)[:, None]
    earlier = jnp.arange(blocks)[None, :]
    distance = jnp.maximum(later - 1 - earlier, 0).astype(jnp.float32)
    carry = jnp.where(
        (earlier < later)[:, :, None, None],
        jnp.exp(-decay[None, None] * (block_len * distance)[:, :, None, None]),
        0.0,
    )
    starts = jnp.sum(carry * block_sums[None], axis=1)
    outer = jnp.einsum("mic,bmc->bic", amplitude[:, None, :] * falloff, starts, precision=precise)
    conv = (inner + outer).reshape(length, sub)
    gated = (short[:, 0, :] * (conv + skip[None, :] * product)).astype(jnp.bfloat16)
    gated = lax.all_to_all(gated, "seq", 0, 1, tiled=True)
    opposite = lax.ppermute(gated, "zhi", [(z, outer_n - 1 - z) for z in range(outer_n)])
    pair = jnp.where(far == 0, jnp.stack([gated, opposite], 1), jnp.stack([opposite, gated], 1))
    whole = lax.all_gather(pair, "inner", axis=2, tiled=False)
    mixed = jnp.dot(
        whole.reshape(tok_rows, ten_n * channels),
        out_weight,
        preferred_element_type=jnp.float32,
    )
    return mixed.astype(jnp.bfloat16)


def solution(mesh):
    devices = mesh.devices
    halves_mesh = jax.sharding.Mesh(
        devices.reshape(devices.shape[0], devices.shape[1], 2, devices.shape[2] // 2),
        ("dp", "seq", "zhi", "inner"),
    )
    tensor = ("zhi", "inner")
    in_specs = (
        P(("dp", "seq"), tensor),
        P("seq", None, tensor),
        P(None, None, tensor),
        P(None, tensor),
        P(None, tensor),
        P(tensor),
        P(None, tensor),
    )
    out_specs = P(("dp", "seq"), tensor)
    return jax.shard_map(
        body, mesh=halves_mesh, in_specs=in_specs, out_specs=out_specs, check_vma=False
    )
```

```python
import jax
import jax.numpy as jnp
from jax import lax
from jax.sharding import PartitionSpec as P

precise = lax.Precision.HIGHEST
block_len = 64


def body(features, in_weight, short_taps, decay_rates, residues, skip_gain, out_weight):
    seq_n = lax.axis_size("seq")
    outer_n = lax.axis_size("zhi")
    inner_n = lax.axis_size("inner")
    ten_n = outer_n * inner_n
    place = lax.axis_index("seq")
    far = lax.axis_index("zhi")
    lane = far * inner_n + lax.axis_index("inner")
    tok_rows, fcols = features.shape
    rows_here, branches, channels = in_weight.shape
    halves = rows_here // fcols
    sub = channels // seq_n
    length = tok_rows * seq_n
    taps_count = short_taps.shape[1]
    copies = jnp.tile(features, (seq_n, 1))
    my_columns = lax.all_to_all(copies, "seq", 0, 0, tiled=True)
    across = []
    for s in range(seq_n):
        for a in range(seq_n):
            for b in range(halves):
                across.append((a * ten_n + s * halves + b, s * ten_n + a * halves + b))
    first = lax.ppermute(my_columns, ("seq", "zhi", "inner"), across)
    swap = [(k, k + 1 - 2 * (k % 2)) for k in range(inner_n)]
    second = lax.ppermute(first, "inner", swap)
    rows_of_feats = jnp.concatenate([first, second], axis=1)
    half_of = lane % halves
    doubled = jnp.concatenate([in_weight, in_weight], axis=0)
    weight_rows = lax.dynamic_slice_in_dim(doubled, half_of * fcols, rows_here, axis=0)
    weight_rows = weight_rows.reshape(rows_here, branches, seq_n, sub).transpose(0, 1, 3, 2)
    partial = jnp.einsum(
        "djcg,td->jcgt", weight_rows, rows_of_feats, preferred_element_type=jnp.float32
    )
    summed = lax.psum_scatter(
        partial.reshape(branches * sub, seq_n * length), "seq", scatter_dimension=1, tiled=True
    )
    summed = summed.T.reshape(length, branches, sub)
    projected = lax.reduce_precision(summed, exponent_bits=8, mantissa_bits=7)

    taps = lax.dynamic_slice_in_dim(short_taps, place * sub, sub, axis=2)
    decay = lax.dynamic_slice_in_dim(decay_rates, place * sub, sub, axis=1)
    resid = lax.dynamic_slice_in_dim(residues, place * sub, sub, axis=1)
    skip = lax.dynamic_slice_in_dim(skip_gain, place * sub, sub, axis=0)

    rim_rows = taps_count - 1
    extended = jnp.concatenate(
        [jnp.zeros((rim_rows, branches, sub), jnp.float32), projected], axis=0
    )
    short = jnp.zeros((length, branches, sub), jnp.float32)
    for offset_lag in range(taps_count):
        short = (
            short
            + taps[:, offset_lag, :][None]
            * extended[rim_rows - offset_lag : rim_rows - offset_lag + length]
        )
    product = short[:, 1, :] * short[:, 2, :]
    blocks = length // block_len
    pieces = product.reshape(blocks, block_len, sub)
    amplitude = resid * jnp.sqrt(2.0 * decay)
    offsets = jnp.arange(block_len).astype(jnp.float32)
    falloff = jnp.exp(-decay[:, None, :] * offsets[None, :, None])
    kernel = jnp.einsum("mc,mtc->tc", amplitude, falloff, precision=precise)
    lag_grid = jnp.arange(block_len)[:, None] - jnp.arange(block_len)[None, :]
    select = (lag_grid[:, :, None] == jnp.arange(block_len)[None, None, :]).astype(jnp.float32)
    toeplitz = jnp.einsum("tsk,kc->tsc", select, kernel, precision=precise)
    inner = jnp.einsum("tsc,bsc->btc", toeplitz, pieces, precision=precise)
    toward_end = jnp.exp(-decay[:, None, :] * (block_len - offsets)[None, :, None])
    block_sums = jnp.einsum("msc,bsc->bmc", toward_end, pieces, precision=precise)
    later = jnp.arange(blocks)[:, None]
    earlier = jnp.arange(blocks)[None, :]
    distance = jnp.maximum(later - 1 - earlier, 0).astype(jnp.float32)
    carry = jnp.where(
        (earlier < later)[:, :, None, None],
        jnp.exp(-decay[None, None] * (block_len * distance)[:, :, None, None]),
        0.0,
    )
    starts = jnp.sum(carry * block_sums[None], axis=1)
    outer = jnp.einsum("mic,bmc->bic", amplitude[:, None, :] * falloff, starts, precision=precise)
    conv = (inner + outer).reshape(length, sub)
    gated = (short[:, 0, :] * (conv + skip[None, :] * product)).astype(jnp.bfloat16)
    gated = lax.all_to_all(gated, "seq", 0, 1, tiled=True)
    opposite = lax.ppermute(gated, "zhi", [(z, outer_n - 1 - z) for z in range(outer_n)])
    pair = jnp.where(far == 0, jnp.stack([gated, opposite], 1), jnp.stack([opposite, gated], 1))
    whole = lax.all_gather(pair, "inner", axis=2, tiled=False)
    mixed = jnp.dot(
        whole.reshape(tok_rows, ten_n * channels),
        out_weight,
        preferred_element_type=jnp.float32,
    )
    return mixed.astype(jnp.bfloat16)


def solution(mesh):
    devices = mesh.devices
    halves_mesh = jax.sharding.Mesh(
        devices.reshape(devices.shape[0], devices.shape[1], 2, devices.shape[2] // 2),
        ("dp", "seq", "zhi", "inner"),
    )
    tensor = ("zhi", "inner")
    in_specs = (
        P(("dp", "seq"), tensor),
        P("seq", None, tensor),
        P(None, None, tensor),
        P(None, tensor),
        P(None, tensor),
        P(tensor),
        P(None, tensor),
    )
    out_specs = P(("dp", "seq"), tensor)
    return jax.shard_map(
        body, mesh=halves_mesh, in_specs=in_specs, out_specs=out_specs, check_vma=False
    )
```

```python
import jax
import jax.numpy as jnp
from jax import lax
from jax.sharding import PartitionSpec as P

precise = lax.Precision.HIGHEST
block_len = 64


def body(features, in_weight, short_taps, decay_rates, residues, skip_gain, out_weight):
    seq_n = lax.axis_size("seq")
    outer_n = lax.axis_size("zhi")
    inner_n = lax.axis_size("inner")
    ten_n = outer_n * inner_n
    place = lax.axis_index("seq")
    far = lax.axis_index("zhi")
    lane = far * inner_n + lax.axis_index("inner")
    tok_rows, fcols = features.shape
    rows_here, branches, channels = in_weight.shape
    halves = rows_here // fcols
    sub = channels // seq_n
    length = tok_rows * seq_n
    taps_count = short_taps.shape[1]
    copies = jnp.tile(features, (seq_n, 1))
    my_columns = lax.all_to_all(copies, "seq", 0, 0, tiled=True)
    across = []
    for s in range(seq_n):
        for a in range(seq_n):
            for b in range(halves):
                across.append((a * ten_n + s * halves + b, s * ten_n + a * halves + b))
    first = lax.ppermute(my_columns, ("seq", "zhi", "inner"), across)
    swap = [(k, k + 1 - 2 * (k % 2)) for k in range(inner_n)]
    second = lax.ppermute(first, "inner", swap)
    rows_of_feats = jnp.concatenate([first, second], axis=1)
    half_of = lane % halves
    doubled = jnp.concatenate([in_weight, in_weight], axis=0)
    weight_rows = lax.dynamic_slice_in_dim(doubled, half_of * fcols, rows_here, axis=0)
    weight_rows = weight_rows.reshape(rows_here, branches, seq_n, sub).transpose(0, 2, 1, 3)
    partial = jnp.einsum(
        "dgjc,td->gjct", weight_rows, rows_of_feats, preferred_element_type=jnp.float32
    )
    summed = lax.psum_scatter(
        partial.reshape(seq_n, branches * sub, length), "seq", scatter_dimension=0, tiled=True
    )
    summed = summed.reshape(branches * sub, length).T.reshape(length, branches, sub)
    projected = lax.reduce_precision(summed, exponent_bits=8, mantissa_bits=7)

    taps = lax.dynamic_slice_in_dim(short_taps, place * sub, sub, axis=2)
    decay = lax.dynamic_slice_in_dim(decay_rates, place * sub, sub, axis=1)
    resid = lax.dynamic_slice_in_dim(residues, place * sub, sub, axis=1)
    skip = lax.dynamic_slice_in_dim(skip_gain, place * sub, sub, axis=0)

    rim_rows = taps_count - 1
    extended = jnp.concatenate(
        [jnp.zeros((rim_rows, branches, sub), jnp.float32), projected], axis=0
    )
    short = jnp.zeros((length, branches, sub), jnp.float32)
    for offset_lag in range(taps_count):
        short = (
            short
            + taps[:, offset_lag, :][None]
            * extended[rim_rows - offset_lag : rim_rows - offset_lag + length]
        )
    product = short[:, 1, :] * short[:, 2, :]
    blocks = length // block_len
    pieces = product.reshape(blocks, block_len, sub)
    amplitude = resid * jnp.sqrt(2.0 * decay)
    offsets = jnp.arange(block_len).astype(jnp.float32)
    falloff = jnp.exp(-decay[:, None, :] * offsets[None, :, None])
    kernel = jnp.einsum("mc,mtc->tc", amplitude, falloff, precision=precise)
    lag_grid = jnp.arange(block_len)[:, None] - jnp.arange(block_len)[None, :]
    select = (lag_grid[:, :, None] == jnp.arange(block_len)[None, None, :]).astype(jnp.float32)
    toeplitz = jnp.einsum("tsk,kc->tsc", select, kernel, precision=precise)
    inner = jnp.einsum("tsc,bsc->btc", toeplitz, pieces, precision=precise)
    toward_end = jnp.exp(-decay[:, None, :] * (block_len - offsets)[None, :, None])
    block_sums = jnp.einsum("msc,bsc->bmc", toward_end, pieces, precision=precise)
    later = jnp.arange(blocks)[:, None]
    earlier = jnp.arange(blocks)[None, :]
    distance = jnp.maximum(later - 1 - earlier, 0).astype(jnp.float32)
    carry = jnp.where(
        (earlier < later)[:, :, None, None],
        jnp.exp(-decay[None, None] * (block_len * distance)[:, :, None, None]),
        0.0,
    )
    starts = jnp.sum(carry * block_sums[None], axis=1)
    outer = jnp.einsum("mic,bmc->bic", amplitude[:, None, :] * falloff, starts, precision=precise)
    conv = (inner + outer).reshape(length, sub)
    gated = (short[:, 0, :] * (conv + skip[None, :] * product)).astype(jnp.bfloat16)
    gated = lax.all_to_all(gated, "seq", 0, 1, tiled=True)
    opposite = lax.ppermute(gated, "zhi", [(z, outer_n - 1 - z) for z in range(outer_n)])
    pair = jnp.where(far == 0, jnp.stack([gated, opposite], 1), jnp.stack([opposite, gated], 1))
    whole = lax.all_gather(pair, "inner", axis=2, tiled=False)
    mixed = jnp.dot(
        whole.reshape(tok_rows, ten_n * channels),
        out_weight,
        preferred_element_type=jnp.float32,
    )
    return mixed.astype(jnp.bfloat16)


def solution(mesh):
    devices = mesh.devices
    halves_mesh = jax.sharding.Mesh(
        devices.reshape(devices.shape[0], devices.shape[1], 2, devices.shape[2] // 2),
        ("dp", "seq", "zhi", "inner"),
    )
    tensor = ("zhi", "inner")
    in_specs = (
        P(("dp", "seq"), tensor),
        P("seq", None, tensor),
        P(None, None, tensor),
        P(None, tensor),
        P(None, tensor),
        P(tensor),
        P(None, tensor),
    )
    out_specs = P(("dp", "seq"), tensor)
    return jax.shard_map(
        body, mesh=halves_mesh, in_specs=in_specs, out_specs=out_specs, check_vma=False
    )
```

```python
import jax
import jax.numpy as jnp
from jax import lax
from jax.sharding import PartitionSpec as P

precise = lax.Precision.HIGHEST
block_len = 64


def body(features, in_weight, short_taps, decay_rates, residues, skip_gain, out_weight):
    seq_n = lax.axis_size("seq")
    outer_n = lax.axis_size("zhi")
    inner_n = lax.axis_size("inner")
    ten_n = outer_n * inner_n
    place = lax.axis_index("seq")
    far = lax.axis_index("zhi")
    lane = far * inner_n + lax.axis_index("inner")
    tok_rows, fcols = features.shape
    rows_here, branches, channels = in_weight.shape
    halves = rows_here // fcols
    sub = channels // seq_n
    length = tok_rows * seq_n
    taps_count = short_taps.shape[1]
    copies = jnp.tile(features, (seq_n, 1))
    my_columns = lax.all_to_all(copies, "seq", 0, 0, tiled=True)
    across = []
    for s in range(seq_n):
        for a in range(seq_n):
            for b in range(halves):
                across.append((a * ten_n + s * halves + b, s * ten_n + a * halves + b))
    first = lax.ppermute(my_columns, ("seq", "zhi", "inner"), across)
    swap = [(k, k + 1 - 2 * (k % 2)) for k in range(inner_n)]
    second = lax.ppermute(first, "inner", swap)
    rows_of_feats = jnp.concatenate([first, second], axis=1)
    half_of = lane % halves
    doubled = jnp.concatenate([in_weight, in_weight], axis=0)
    weight_rows = lax.dynamic_slice_in_dim(doubled, half_of * fcols, rows_here, axis=0)
    weight_rows = weight_rows.reshape(rows_here, branches, seq_n, sub).transpose(0, 2, 1, 3)
    partial = jnp.einsum(
        "dgjc,td->gjct", weight_rows, rows_of_feats, preferred_element_type=jnp.float32
    )
    summed = lax.psum_scatter(
        partial.reshape(seq_n, branches * sub, length), "seq", scatter_dimension=0, tiled=True
    )
    summed = summed.reshape(branches * sub, length).T.reshape(length, branches, sub)
    projected = lax.reduce_precision(summed, exponent_bits=8, mantissa_bits=7)

    taps = lax.dynamic_slice_in_dim(short_taps, place * sub, sub, axis=2)
    decay = lax.dynamic_slice_in_dim(decay_rates, place * sub, sub, axis=1)
    resid = lax.dynamic_slice_in_dim(residues, place * sub, sub, axis=1)
    skip = lax.dynamic_slice_in_dim(skip_gain, place * sub, sub, axis=0)

    rim_rows = taps_count - 1
    extended = jnp.concatenate(
        [jnp.zeros((rim_rows, branches, sub), jnp.float32), projected], axis=0
    )
    short = jnp.zeros((length, branches, sub), jnp.float32)
    for offset_lag in range(taps_count):
        short = (
            short
            + taps[:, offset_lag, :][None]
            * extended[rim_rows - offset_lag : rim_rows - offset_lag + length]
        )
    product = short[:, 1, :] * short[:, 2, :]
    blocks = length // block_len
    pieces = product.reshape(blocks, block_len, sub)
    amplitude = resid * jnp.sqrt(2.0 * decay)
    offsets = jnp.arange(block_len).astype(jnp.float32)
    falloff = jnp.exp(-decay[:, None, :] * offsets[None, :, None])
    kernel = jnp.einsum("mc,mtc->tc", amplitude, falloff, precision=precise)
    lag_grid = jnp.arange(block_len)[:, None] - jnp.arange(block_len)[None, :]
    select = (lag_grid[:, :, None] == jnp.arange(block_len)[None, None, :]).astype(jnp.float32)
    toeplitz = jnp.einsum("tsk,kc->tsc", select, kernel, precision=precise)
    inner = jnp.einsum("tsc,bsc->btc", toeplitz, pieces, precision=precise)
    toward_end = jnp.exp(-decay[:, None, :] * (block_len - offsets)[None, :, None])
    block_sums = jnp.einsum("msc,bsc->bmc", toward_end, pieces, precision=precise)
    later = jnp.arange(blocks)[:, None]
    earlier = jnp.arange(blocks)[None, :]
    distance = jnp.maximum(later - 1 - earlier, 0).astype(jnp.float32)
    carry = jnp.where(
        (earlier < later)[:, :, None, None],
        jnp.exp(-decay[None, None] * (block_len * distance)[:, :, None, None]),
        0.0,
    )
    starts = jnp.sum(carry * block_sums[None], axis=1)
    outer = jnp.einsum("mic,bmc->bic", amplitude[:, None, :] * falloff, starts, precision=precise)
    conv = (inner + outer).reshape(length, sub)
    gated = (short[:, 0, :] * (conv + skip[None, :] * product)).astype(jnp.bfloat16)
    outgoing = jnp.broadcast_to(
        gated.reshape(seq_n, 1, tok_rows, sub), (seq_n, outer_n, tok_rows, sub)
    ).reshape(seq_n * outer_n * tok_rows, sub)
    incoming = lax.all_to_all(outgoing, ("seq", "zhi"), 0, 0, tiled=True)
    pair = incoming.reshape(seq_n, outer_n, tok_rows, sub).transpose(2, 1, 0, 3)
    pair = pair.reshape(tok_rows, outer_n, seq_n * sub)
    whole = lax.all_gather(pair, "inner", axis=2, tiled=False)
    mixed = jnp.dot(
        whole.reshape(tok_rows, ten_n * channels),
        out_weight,
        preferred_element_type=jnp.float32,
    )
    return mixed.astype(jnp.bfloat16)


def solution(mesh):
    devices = mesh.devices
    halves_mesh = jax.sharding.Mesh(
        devices.reshape(devices.shape[0], devices.shape[1], 2, devices.shape[2] // 2),
        ("dp", "seq", "zhi", "inner"),
    )
    tensor = ("zhi", "inner")
    in_specs = (
        P(("dp", "seq"), tensor),
        P("seq", None, tensor),
        P(None, None, tensor),
        P(None, tensor),
        P(None, tensor),
        P(tensor),
        P(None, tensor),
    )
    out_specs = P(("dp", "seq"), tensor)
    return jax.shard_map(
        body, mesh=halves_mesh, in_specs=in_specs, out_specs=out_specs, check_vma=False
    )
```

```python
import jax
import jax.numpy as jnp
from jax import lax
from jax.sharding import PartitionSpec as P

precise = lax.Precision.HIGHEST
block_len = 64


def body(features, in_weight, short_taps, decay_rates, residues, skip_gain, out_weight):
    seq_n = lax.axis_size("seq")
    outer_n = lax.axis_size("zhi")
    inner_n = lax.axis_size("inner")
    ten_n = outer_n * inner_n
    place = lax.axis_index("seq")
    far = lax.axis_index("zhi")
    lane = far * inner_n + lax.axis_index("inner")
    tok_rows, fcols = features.shape
    rows_here, branches, channels = in_weight.shape
    halves = rows_here // fcols
    sub = channels // seq_n
    length = tok_rows * seq_n
    taps_count = short_taps.shape[1]
    flip = []
    for s in range(seq_n):
        for c in range(seq_n):
            for e in range(halves):
                flip.append((s * ten_n + c * halves + e, c * ten_n + s * halves + e))
    flipped = lax.ppermute(features, ("seq", "zhi", "inner"), flip)
    copies = jnp.tile(flipped, (ten_n, 1))
    gathered = lax.all_to_all(copies, ("zhi", "inner"), 0, 1, tiled=True)
    rows_of_feats = (
        gathered.reshape(tok_rows, seq_n, halves * fcols)
        .transpose(1, 0, 2)
        .reshape(length, rows_here)
    )
    weight_rows = in_weight.reshape(rows_here, branches, seq_n, sub).transpose(0, 2, 1, 3)
    partial = jnp.einsum(
        "dgjc,td->gjct", weight_rows, rows_of_feats, preferred_element_type=jnp.float32
    )
    summed = lax.psum_scatter(
        partial.reshape(seq_n, branches * sub, length), "seq", scatter_dimension=0, tiled=True
    )
    summed = summed.reshape(branches * sub, length).T.reshape(length, branches, sub)
    projected = lax.reduce_precision(summed, exponent_bits=8, mantissa_bits=7)

    taps = lax.dynamic_slice_in_dim(short_taps, place * sub, sub, axis=2)
    decay = lax.dynamic_slice_in_dim(decay_rates, place * sub, sub, axis=1)
    resid = lax.dynamic_slice_in_dim(residues, place * sub, sub, axis=1)
    skip = lax.dynamic_slice_in_dim(skip_gain, place * sub, sub, axis=0)

    rim_rows = taps_count - 1
    extended = jnp.concatenate(
        [jnp.zeros((rim_rows, branches, sub), jnp.float32), projected], axis=0
    )
    short = jnp.zeros((length, branches, sub), jnp.float32)
    for offset_lag in range(taps_count):
        short = (
            short
            + taps[:, offset_lag, :][None]
            * extended[rim_rows - offset_lag : rim_rows - offset_lag + length]
        )
    product = short[:, 1, :] * short[:, 2, :]
    blocks = length // block_len
    pieces = product.reshape(blocks, block_len, sub)
    amplitude = resid * jnp.sqrt(2.0 * decay)
    offsets = jnp.arange(block_len).astype(jnp.float32)
    falloff = jnp.exp(-decay[:, None, :] * offsets[None, :, None])
    kernel = jnp.einsum("mc,mtc->tc", amplitude, falloff, precision=precise)
    lag_grid = jnp.arange(block_len)[:, None] - jnp.arange(block_len)[None, :]
    select = (lag_grid[:, :, None] == jnp.arange(block_len)[None, None, :]).astype(jnp.float32)
    toeplitz = jnp.einsum("tsk,kc->tsc", select, kernel, precision=precise)
    inner = jnp.einsum("tsc,bsc->btc", toeplitz, pieces, precision=precise)
    toward_end = jnp.exp(-decay[:, None, :] * (block_len - offsets)[None, :, None])
    block_sums = jnp.einsum("msc,bsc->bmc", toward_end, pieces, precision=precise)
    later = jnp.arange(blocks)[:, None]
    earlier = jnp.arange(blocks)[None, :]
    distance = jnp.maximum(later - 1 - earlier, 0).astype(jnp.float32)
    carry = jnp.where(
        (earlier < later)[:, :, None, None],
        jnp.exp(-decay[None, None] * (block_len * distance)[:, :, None, None]),
        0.0,
    )
    starts = jnp.sum(carry * block_sums[None], axis=1)
    outer = jnp.einsum("mic,bmc->bic", amplitude[:, None, :] * falloff, starts, precision=precise)
    conv = (inner + outer).reshape(length, sub)
    gated = (short[:, 0, :] * (conv + skip[None, :] * product)).astype(jnp.bfloat16)
    outgoing = jnp.broadcast_to(
        gated.reshape(seq_n, 1, tok_rows, sub), (seq_n, outer_n, tok_rows, sub)
    ).reshape(seq_n * outer_n * tok_rows, sub)
    incoming = lax.all_to_all(outgoing, ("seq", "zhi"), 0, 0, tiled=True)
    pair = incoming.reshape(seq_n, outer_n, tok_rows, sub).transpose(2, 1, 0, 3)
    pair = pair.reshape(tok_rows, outer_n, seq_n * sub)
    whole = lax.all_gather(pair, "inner", axis=2, tiled=False)
    mixed = jnp.dot(
        whole.reshape(tok_rows, ten_n * channels),
        out_weight,
        preferred_element_type=jnp.float32,
    )
    return mixed.astype(jnp.bfloat16)


def solution(mesh):
    devices = mesh.devices
    halves_mesh = jax.sharding.Mesh(
        devices.reshape(devices.shape[0], devices.shape[1], 2, devices.shape[2] // 2),
        ("dp", "seq", "zhi", "inner"),
    )
    tensor = ("zhi", "inner")
    in_specs = (
        P(("dp", "seq"), tensor),
        P("seq", None, tensor),
        P(None, None, tensor),
        P(None, tensor),
        P(None, tensor),
        P(tensor),
        P(None, tensor),
    )
    out_specs = P(("dp", "seq"), tensor)
    return jax.shard_map(
        body, mesh=halves_mesh, in_specs=in_specs, out_specs=out_specs, check_vma=False
    )
```

```python
import jax
import jax.numpy as jnp
from jax import lax
from jax.sharding import PartitionSpec as P

precise = lax.Precision.HIGHEST
block_len = 64


def body(features, in_weight, short_taps, decay_rates, residues, skip_gain, out_weight):
    seq_n = lax.axis_size("seq")
    outer_n = lax.axis_size("zhi")
    inner_n = lax.axis_size("inner")
    ten_n = outer_n * inner_n
    place = lax.axis_index("seq")
    far = lax.axis_index("zhi")
    lane = far * inner_n + lax.axis_index("inner")
    tok_rows, fcols = features.shape
    rows_here, branches, channels = in_weight.shape
    halves = rows_here // fcols
    sub = channels // seq_n
    length = tok_rows * seq_n
    taps_count = short_taps.shape[1]
    y_n = inner_n // halves

    def mirror(c):
        return (outer_n - 1 - c // y_n) * y_n + c % y_n

    flip, flip_far = [], []
    for s in range(seq_n):
        for c in range(seq_n):
            for e in range(halves):
                flip.append((s * ten_n + c * halves + e, c * ten_n + s * halves + e))
                flip_far.append((s * ten_n + c * halves + e, c * ten_n + mirror(s) * halves + e))
    near = lax.ppermute(features, ("seq", "zhi", "inner"), flip)
    away = lax.ppermute(features, ("seq", "zhi", "inner"), flip_far)
    pair = jnp.where(far == 0, jnp.stack([near, away]), jnp.stack([away, near]))
    gathered = lax.all_gather(pair, "inner", axis=0, tiled=False)
    rows_of_feats = (
        gathered.reshape(y_n, halves, outer_n, tok_rows, fcols)
        .transpose(2, 0, 3, 1, 4)
        .reshape(length, rows_here)
    )
    weight_rows = in_weight.reshape(rows_here, branches, seq_n, sub).transpose(0, 2, 1, 3)
    partial = jnp.einsum(
        "dgjc,td->gjct", weight_rows, rows_of_feats, preferred_element_type=jnp.float32
    )
    summed = lax.psum_scatter(
        partial.reshape(seq_n, branches * sub, length), "seq", scatter_dimension=0, tiled=True
    )
    summed = summed.reshape(branches * sub, length).T.reshape(length, branches, sub)
    projected = lax.reduce_precision(summed, exponent_bits=8, mantissa_bits=7)

    taps = lax.dynamic_slice_in_dim(short_taps, place * sub, sub, axis=2)
    decay = lax.dynamic_slice_in_dim(decay_rates, place * sub, sub, axis=1)
    resid = lax.dynamic_slice_in_dim(residues, place * sub, sub, axis=1)
    skip = lax.dynamic_slice_in_dim(skip_gain, place * sub, sub, axis=0)

    rim_rows = taps_count - 1
    extended = jnp.concatenate(
        [jnp.zeros((rim_rows, branches, sub), jnp.float32), projected], axis=0
    )
    short = jnp.zeros((length, branches, sub), jnp.float32)
    for offset_lag in range(taps_count):
        short = (
            short
            + taps[:, offset_lag, :][None]
            * extended[rim_rows - offset_lag : rim_rows - offset_lag + length]
        )
    product = short[:, 1, :] * short[:, 2, :]
    blocks = length // block_len
    pieces = product.reshape(blocks, block_len, sub)
    amplitude = resid * jnp.sqrt(2.0 * decay)
    offsets = jnp.arange(block_len).astype(jnp.float32)
    falloff = jnp.exp(-decay[:, None, :] * offsets[None, :, None])
    kernel = jnp.einsum("mc,mtc->tc", amplitude, falloff, precision=precise)
    lag_grid = jnp.arange(block_len)[:, None] - jnp.arange(block_len)[None, :]
    select = (lag_grid[:, :, None] == jnp.arange(block_len)[None, None, :]).astype(jnp.float32)
    toeplitz = jnp.einsum("tsk,kc->tsc", select, kernel, precision=precise)
    inner = jnp.einsum("tsc,bsc->btc", toeplitz, pieces, precision=precise)
    toward_end = jnp.exp(-decay[:, None, :] * (block_len - offsets)[None, :, None])
    block_sums = jnp.einsum("msc,bsc->bmc", toward_end, pieces, precision=precise)
    later = jnp.arange(blocks)[:, None]
    earlier = jnp.arange(blocks)[None, :]
    distance = jnp.maximum(later - 1 - earlier, 0).astype(jnp.float32)
    carry = jnp.where(
        (earlier < later)[:, :, None, None],
        jnp.exp(-decay[None, None] * (block_len * distance)[:, :, None, None]),
        0.0,
    )
    starts = jnp.sum(carry * block_sums[None], axis=1)
    outer = jnp.einsum("mic,bmc->bic", amplitude[:, None, :] * falloff, starts, precision=precise)
    conv = (inner + outer).reshape(length, sub)
    gated = (short[:, 0, :] * (conv + skip[None, :] * product)).astype(jnp.bfloat16)
    outgoing = jnp.broadcast_to(
        gated.reshape(seq_n, 1, tok_rows, sub), (seq_n, outer_n, tok_rows, sub)
    ).reshape(seq_n * outer_n * tok_rows, sub)
    incoming = lax.all_to_all(outgoing, ("seq", "zhi"), 0, 0, tiled=True)
    pair = incoming.reshape(seq_n, outer_n, tok_rows, sub).transpose(2, 1, 0, 3)
    pair = pair.reshape(tok_rows, outer_n, seq_n * sub)
    whole = lax.all_gather(pair, "inner", axis=2, tiled=False)
    mixed = jnp.dot(
        whole.reshape(tok_rows, ten_n * channels),
        out_weight,
        preferred_element_type=jnp.float32,
    )
    return mixed.astype(jnp.bfloat16)


def solution(mesh):
    devices = mesh.devices
    halves_mesh = jax.sharding.Mesh(
        devices.reshape(devices.shape[0], devices.shape[1], 2, devices.shape[2] // 2),
        ("dp", "seq", "zhi", "inner"),
    )
    tensor = ("zhi", "inner")
    in_specs = (
        P(("dp", "seq"), tensor),
        P("seq", None, tensor),
        P(None, None, tensor),
        P(None, tensor),
        P(None, tensor),
        P(tensor),
        P(None, tensor),
    )
    out_specs = P(("dp", "seq"), tensor)
    return jax.shard_map(
        body, mesh=halves_mesh, in_specs=in_specs, out_specs=out_specs, check_vma=False
    )
```

```python
import jax
import jax.numpy as jnp
from jax import lax
from jax.sharding import PartitionSpec as P

precise = lax.Precision.HIGHEST
block_len = 64


def body(features, in_weight, short_taps, decay_rates, residues, skip_gain, out_weight):
    seq_n = lax.axis_size("seq")
    outer_n = lax.axis_size("zhi")
    inner_n = lax.axis_size("inner")
    ten_n = outer_n * inner_n
    place = lax.axis_index("seq")
    far = lax.axis_index("zhi")
    lane = far * inner_n + lax.axis_index("inner")
    tok_rows, fcols = features.shape
    rows_here, branches, channels = in_weight.shape
    halves = rows_here // fcols
    sub = channels // seq_n
    length = tok_rows * seq_n
    taps_count = short_taps.shape[1]
    routes = [[], []]
    for s in range(seq_n):
        for c in range(seq_n):
            for e in range(halves):
                for h in range(outer_n):
                    src_id = s * ten_n + c * halves + e
                    dst_id = c * ten_n + h * inner_n + s
                    routes[(e + h) % 2].append((src_id, dst_id))
    first = lax.ppermute(features, ("seq", "zhi", "inner"), routes[0])
    second = lax.ppermute(features, ("seq", "zhi", "inner"), routes[1])
    col_lo = jnp.where(far == 0, first, second)
    col_hi = jnp.where(far == 0, second, first)
    pair = jnp.concatenate([col_lo, col_hi], axis=1)
    gathered = lax.all_gather(pair, "inner", axis=0, tiled=True)
    rows_of_feats = gathered.reshape(length, rows_here)
    weight_rows = in_weight.reshape(rows_here, branches, seq_n, sub).transpose(0, 2, 1, 3)
    partial = jnp.einsum(
        "dgjc,td->gjct", weight_rows, rows_of_feats, preferred_element_type=jnp.float32
    )
    summed = lax.psum_scatter(
        partial.reshape(seq_n, branches * sub, length), "seq", scatter_dimension=0, tiled=True
    )
    summed = summed.reshape(branches * sub, length).T.reshape(length, branches, sub)
    projected = lax.reduce_precision(summed, exponent_bits=8, mantissa_bits=7)

    taps = lax.dynamic_slice_in_dim(short_taps, place * sub, sub, axis=2)
    decay = lax.dynamic_slice_in_dim(decay_rates, place * sub, sub, axis=1)
    resid = lax.dynamic_slice_in_dim(residues, place * sub, sub, axis=1)
    skip = lax.dynamic_slice_in_dim(skip_gain, place * sub, sub, axis=0)

    rim_rows = taps_count - 1
    extended = jnp.concatenate(
        [jnp.zeros((rim_rows, branches, sub), jnp.float32), projected], axis=0
    )
    short = jnp.zeros((length, branches, sub), jnp.float32)
    for offset_lag in range(taps_count):
        short = (
            short
            + taps[:, offset_lag, :][None]
            * extended[rim_rows - offset_lag : rim_rows - offset_lag + length]
        )
    product = short[:, 1, :] * short[:, 2, :]
    blocks = length // block_len
    pieces = product.reshape(blocks, block_len, sub)
    amplitude = resid * jnp.sqrt(2.0 * decay)
    offsets = jnp.arange(block_len).astype(jnp.float32)
    falloff = jnp.exp(-decay[:, None, :] * offsets[None, :, None])
    kernel = jnp.einsum("mc,mtc->tc", amplitude, falloff, precision=precise)
    lag_grid = jnp.arange(block_len)[:, None] - jnp.arange(block_len)[None, :]
    select = (lag_grid[:, :, None] == jnp.arange(block_len)[None, None, :]).astype(jnp.float32)
    toeplitz = jnp.einsum("tsk,kc->tsc", select, kernel, precision=precise)
    inner = jnp.einsum("tsc,bsc->btc", toeplitz, pieces, precision=precise)
    toward_end = jnp.exp(-decay[:, None, :] * (block_len - offsets)[None, :, None])
    block_sums = jnp.einsum("msc,bsc->bmc", toward_end, pieces, precision=precise)
    later = jnp.arange(blocks)[:, None]
    earlier = jnp.arange(blocks)[None, :]
    distance = jnp.maximum(later - 1 - earlier, 0).astype(jnp.float32)
    carry = jnp.where(
        (earlier < later)[:, :, None, None],
        jnp.exp(-decay[None, None] * (block_len * distance)[:, :, None, None]),
        0.0,
    )
    starts = jnp.sum(carry * block_sums[None], axis=1)
    outer = jnp.einsum("mic,bmc->bic", amplitude[:, None, :] * falloff, starts, precision=precise)
    conv = (inner + outer).reshape(length, sub)
    gated = (short[:, 0, :] * (conv + skip[None, :] * product)).astype(jnp.bfloat16)
    outgoing = jnp.broadcast_to(
        gated.reshape(seq_n, 1, tok_rows, sub), (seq_n, outer_n, tok_rows, sub)
    ).reshape(seq_n * outer_n * tok_rows, sub)
    incoming = lax.all_to_all(outgoing, ("seq", "zhi"), 0, 0, tiled=True)
    pair = incoming.reshape(seq_n, outer_n, tok_rows, sub).transpose(2, 1, 0, 3)
    pair = pair.reshape(tok_rows, outer_n, seq_n * sub)
    whole = lax.all_gather(pair, "inner", axis=2, tiled=False)
    mixed = jnp.dot(
        whole.reshape(tok_rows, ten_n * channels),
        out_weight,
        preferred_element_type=jnp.float32,
    )
    return mixed.astype(jnp.bfloat16)


def solution(mesh):
    devices = mesh.devices
    halves_mesh = jax.sharding.Mesh(
        devices.reshape(devices.shape[0], devices.shape[1], 2, devices.shape[2] // 2),
        ("dp", "seq", "zhi", "inner"),
    )
    tensor = ("zhi", "inner")
    in_specs = (
        P(("dp", "seq"), tensor),
        P("seq", None, tensor),
        P(None, None, tensor),
        P(None, tensor),
        P(None, tensor),
        P(tensor),
        P(None, tensor),
    )
    out_specs = P(("dp", "seq"), tensor)
    return jax.shard_map(
        body, mesh=halves_mesh, in_specs=in_specs, out_specs=out_specs, check_vma=False
    )
```

```python
import jax
import jax.numpy as jnp
from jax import lax
from jax.sharding import PartitionSpec as P

precise = lax.Precision.HIGHEST
block_len = 64


def body(features, in_weight, short_taps, decay_rates, residues, skip_gain, out_weight):
    seq_n = lax.axis_size("seq")
    outer_n = lax.axis_size("zhi")
    inner_n = lax.axis_size("inner")
    ten_n = outer_n * inner_n
    place = lax.axis_index("seq")
    far = lax.axis_index("zhi")
    lane = far * inner_n + lax.axis_index("inner")
    tok_rows, fcols = features.shape
    rows_here, branches, channels = in_weight.shape
    halves = rows_here // fcols
    sub = channels // seq_n
    length = tok_rows * seq_n
    taps_count = short_taps.shape[1]
    routes = [[], []]
    for s in range(seq_n):
        for c in range(seq_n):
            for e in range(halves):
                for h in range(outer_n):
                    src_id = s * ten_n + c * halves + e
                    dst_id = c * ten_n + h * inner_n + s
                    routes[(e + h) % 2].append((src_id, dst_id))
    first = lax.ppermute(features, ("seq", "zhi", "inner"), routes[0])
    second = lax.ppermute(features, ("seq", "zhi", "inner"), routes[1])
    col_lo = jnp.where(far == 0, first, second)
    col_hi = jnp.where(far == 0, second, first)
    pair = jnp.concatenate([col_lo, col_hi], axis=1)
    gathered = lax.all_gather(pair, "inner", axis=0, tiled=True)
    rows_of_feats = gathered.reshape(length, rows_here)
    weight_rows = in_weight.reshape(rows_here, branches, seq_n, sub).transpose(0, 2, 1, 3)
    partial = jnp.einsum(
        "dgjc,td->gjct", weight_rows, rows_of_feats, preferred_element_type=jnp.float32
    )
    summed = lax.psum_scatter(
        partial.reshape(seq_n, branches * sub, length), "seq", scatter_dimension=0, tiled=True
    )
    summed = summed.reshape(branches * sub, length).T.reshape(length, branches, sub)
    projected = lax.reduce_precision(summed, exponent_bits=8, mantissa_bits=7)

    taps = lax.dynamic_slice_in_dim(short_taps, place * sub, sub, axis=2)
    decay = lax.dynamic_slice_in_dim(decay_rates, place * sub, sub, axis=1)
    resid = lax.dynamic_slice_in_dim(residues, place * sub, sub, axis=1)
    skip = lax.dynamic_slice_in_dim(skip_gain, place * sub, sub, axis=0)

    rim_rows = taps_count - 1
    extended = jnp.concatenate(
        [jnp.zeros((rim_rows, branches, sub), jnp.float32), projected], axis=0
    )
    short = jnp.zeros((length, branches, sub), jnp.float32)
    for offset_lag in range(taps_count):
        short = (
            short
            + taps[:, offset_lag, :][None]
            * extended[rim_rows - offset_lag : rim_rows - offset_lag + length]
        )
    product = short[:, 1, :] * short[:, 2, :]
    blocks = length // block_len
    pieces = product.reshape(blocks, block_len, sub)
    amplitude = resid * jnp.sqrt(2.0 * decay)
    offsets = jnp.arange(block_len).astype(jnp.float32)
    falloff = jnp.exp(-decay[:, None, :] * offsets[None, :, None])
    kernel = jnp.einsum("mc,mtc->tc", amplitude, falloff, precision=precise)
    lag_grid = jnp.arange(block_len)[:, None] - jnp.arange(block_len)[None, :]
    select = (lag_grid[:, :, None] == jnp.arange(block_len)[None, None, :]).astype(jnp.float32)
    toeplitz = jnp.einsum("tsk,kc->tsc", select, kernel, precision=precise)
    inner = jnp.einsum("tsc,bsc->btc", toeplitz, pieces, precision=precise)
    toward_end = jnp.exp(-decay[:, None, :] * (block_len - offsets)[None, :, None])
    block_sums = jnp.einsum("msc,bsc->bmc", toward_end, pieces, precision=precise)
    later = jnp.arange(blocks)[:, None]
    earlier = jnp.arange(blocks)[None, :]
    distance = jnp.maximum(later - 1 - earlier, 0).astype(jnp.float32)
    carry = jnp.where(
        (earlier < later)[:, :, None, None],
        jnp.exp(-decay[None, None] * (block_len * distance)[:, :, None, None]),
        0.0,
    )
    starts = jnp.sum(carry * block_sums[None], axis=1)
    outer = jnp.einsum("mic,bmc->bic", amplitude[:, None, :] * falloff, starts, precision=precise)
    conv = (inner + outer).reshape(length, sub)
    gated = (short[:, 0, :] * (conv + skip[None, :] * product)).astype(jnp.bfloat16)
    outgoing = jnp.broadcast_to(
        gated.reshape(seq_n, 1, tok_rows, sub), (seq_n, outer_n, tok_rows, sub)
    ).reshape(seq_n * outer_n * tok_rows, sub)
    incoming = lax.all_to_all(outgoing, ("seq", "zhi"), 0, 0, tiled=True)
    pair = incoming.reshape(seq_n, outer_n, tok_rows, sub).transpose(2, 1, 0, 3)
    pair = pair.reshape(tok_rows, outer_n * seq_n * sub)
    whole = lax.all_gather(pair, "inner", axis=1, tiled=True)
    weight_out = (
        out_weight.reshape(outer_n, inner_n, channels, -1)
        .transpose(1, 0, 2, 3)
        .reshape(ten_n * channels, -1)
    )
    mixed = jnp.dot(whole, weight_out, preferred_element_type=jnp.float32)
    return mixed.astype(jnp.bfloat16)


def solution(mesh):
    devices = mesh.devices
    halves_mesh = jax.sharding.Mesh(
        devices.reshape(devices.shape[0], devices.shape[1], 2, devices.shape[2] // 2),
        ("dp", "seq", "zhi", "inner"),
    )
    tensor = ("zhi", "inner")
    in_specs = (
        P(("dp", "seq"), tensor),
        P("seq", None, tensor),
        P(None, None, tensor),
        P(None, tensor),
        P(None, tensor),
        P(tensor),
        P(None, tensor),
    )
    out_specs = P(("dp", "seq"), tensor)
    return jax.shard_map(
        body, mesh=halves_mesh, in_specs=in_specs, out_specs=out_specs, check_vma=False
    )
```

```python
import jax
import jax.numpy as jnp
from jax import lax
from jax.sharding import PartitionSpec as P

precise = lax.Precision.HIGHEST
block_len = 64


def body(features, in_weight, short_taps, decay_rates, residues, skip_gain, out_weight):
    seq_n = lax.axis_size("seq")
    outer_n = lax.axis_size("zhi")
    inner_n = lax.axis_size("inner")
    ten_n = outer_n * inner_n
    place = lax.axis_index("seq")
    far = lax.axis_index("zhi")
    lane = far * inner_n + lax.axis_index("inner")
    tok_rows, fcols = features.shape
    rows_here, branches, channels = in_weight.shape
    halves = rows_here // fcols
    sub = channels // seq_n
    length = tok_rows * seq_n
    taps_count = short_taps.shape[1]
    routes = [[], []]
    for s in range(seq_n):
        for c in range(seq_n):
            for e in range(halves):
                for h in range(outer_n):
                    src_id = s * ten_n + c * halves + e
                    dst_id = c * ten_n + h * inner_n + s
                    routes[(e + h) % 2].append((src_id, dst_id))
    first = lax.ppermute(features, ("seq", "zhi", "inner"), routes[0])
    second = lax.ppermute(features, ("seq", "zhi", "inner"), routes[1])
    col_lo = jnp.where(far == 0, first, second)
    col_hi = jnp.where(far == 0, second, first)
    pair = jnp.concatenate([col_lo, col_hi], axis=1)
    gathered = lax.all_gather(pair, "inner", axis=0, tiled=True)
    rows_of_feats = gathered.reshape(length, rows_here)
    weight_rows = in_weight.reshape(rows_here, branches, seq_n, sub).transpose(0, 2, 1, 3)
    partial = jnp.einsum(
        "dgjc,td->gjct", weight_rows, rows_of_feats, preferred_element_type=jnp.float32
    )
    summed = lax.psum_scatter(
        partial.reshape(seq_n, branches * sub, length), "seq", scatter_dimension=0, tiled=True
    )
    summed = summed.reshape(branches, sub, length)
    projected = lax.reduce_precision(summed, exponent_bits=8, mantissa_bits=7)

    taps = lax.dynamic_slice_in_dim(short_taps, place * sub, sub, axis=2)
    decay = lax.dynamic_slice_in_dim(decay_rates, place * sub, sub, axis=1)
    resid = lax.dynamic_slice_in_dim(residues, place * sub, sub, axis=1)
    skip = lax.dynamic_slice_in_dim(skip_gain, place * sub, sub, axis=0)

    rim_rows = taps_count - 1
    extended = jnp.concatenate(
        [jnp.zeros((branches, sub, rim_rows), jnp.float32), projected], axis=2
    )
    short = jnp.zeros((branches, sub, length), jnp.float32)
    for offset_lag in range(taps_count):
        short = (
            short
            + taps[:, offset_lag, :][:, :, None]
            * extended[:, :, rim_rows - offset_lag : rim_rows - offset_lag + length]
        )
    product = short[1] * short[2]
    blocks = length // block_len
    pieces = product.reshape(sub, blocks, block_len)
    amplitude = resid * jnp.sqrt(2.0 * decay)
    offsets = jnp.arange(block_len).astype(jnp.float32)
    falloff = jnp.exp(-decay[:, :, None] * offsets[None, None, :])
    kernel = jnp.einsum("mc,mct->ct", amplitude, falloff, precision=precise)
    lag_grid = jnp.arange(block_len)[:, None] - jnp.arange(block_len)[None, :]
    select = (lag_grid[:, :, None] == jnp.arange(block_len)[None, None, :]).astype(jnp.float32)
    toeplitz = jnp.einsum("tsk,ck->cts", select, kernel, precision=precise)
    inner = jnp.einsum("cts,cbs->cbt", toeplitz, pieces, precision=precise)
    toward_end = jnp.exp(-decay[:, :, None] * (block_len - offsets)[None, None, :])
    block_sums = jnp.einsum("mcs,cbs->mcb", toward_end, pieces, precision=precise)
    later = jnp.arange(blocks)[:, None]
    earlier = jnp.arange(blocks)[None, :]
    distance = jnp.maximum(later - 1 - earlier, 0).astype(jnp.float32)
    carry = jnp.where(
        (earlier < later)[None, None],
        jnp.exp(-decay[:, :, None, None] * (block_len * distance)[None, None]),
        0.0,
    )
    starts = jnp.sum(carry * block_sums[:, :, None, :], axis=3)
    outer = jnp.einsum("mct,mcb->cbt", amplitude[:, :, None] * falloff, starts, precision=precise)
    conv = (inner + outer).reshape(sub, length)
    gated = (short[0] * (conv + skip[:, None] * product)).astype(jnp.bfloat16).T
    outgoing = jnp.broadcast_to(
        gated.reshape(seq_n, 1, tok_rows, sub), (seq_n, outer_n, tok_rows, sub)
    ).reshape(seq_n * outer_n * tok_rows, sub)
    incoming = lax.all_to_all(outgoing, ("seq", "zhi"), 0, 0, tiled=True)
    pair = incoming.reshape(seq_n, outer_n, tok_rows, sub).transpose(2, 1, 0, 3)
    pair = pair.reshape(tok_rows, outer_n * seq_n * sub)
    whole = lax.all_gather(pair, "inner", axis=1, tiled=True)
    weight_out = (
        out_weight.reshape(outer_n, inner_n, channels, -1)
        .transpose(1, 0, 2, 3)
        .reshape(ten_n * channels, -1)
    )
    mixed = jnp.dot(whole, weight_out, preferred_element_type=jnp.float32)
    return mixed.astype(jnp.bfloat16)


def solution(mesh):
    devices = mesh.devices
    halves_mesh = jax.sharding.Mesh(
        devices.reshape(devices.shape[0], devices.shape[1], 2, devices.shape[2] // 2),
        ("dp", "seq", "zhi", "inner"),
    )
    tensor = ("zhi", "inner")
    in_specs = (
        P(("dp", "seq"), tensor),
        P("seq", None, tensor),
        P(None, None, tensor),
        P(None, tensor),
        P(None, tensor),
        P(tensor),
        P(None, tensor),
    )
    out_specs = P(("dp", "seq"), tensor)
    return jax.shard_map(
        body, mesh=halves_mesh, in_specs=in_specs, out_specs=out_specs, check_vma=False
    )
```

```python
import jax
import jax.numpy as jnp
from jax import lax
from jax.sharding import PartitionSpec as P

precise = lax.Precision.HIGHEST
block_len = 64


def body(features, in_weight, short_taps, decay_rates, residues, skip_gain, out_weight):
    seq_n = lax.axis_size("seq")
    outer_n = lax.axis_size("zhi")
    inner_n = lax.axis_size("inner")
    ten_n = outer_n * inner_n
    place = lax.axis_index("seq")
    far = lax.axis_index("zhi")
    lane = far * inner_n + lax.axis_index("inner")
    tok_rows, fcols = features.shape
    rows_here, branches, channels = in_weight.shape
    halves = rows_here // fcols
    sub = channels // seq_n
    length = tok_rows * seq_n
    taps_count = short_taps.shape[1]
    routes = [[], []]
    for s in range(seq_n):
        for c in range(seq_n):
            for e in range(halves):
                for h in range(outer_n):
                    src_id = s * ten_n + c * halves + e
                    dst_id = c * ten_n + h * inner_n + s
                    routes[(e + h) % 2].append((src_id, dst_id))
    first = lax.ppermute(features, ("seq", "zhi", "inner"), routes[0])
    second = lax.ppermute(features, ("seq", "zhi", "inner"), routes[1])
    col_lo = jnp.where(far == 0, first, second)
    col_hi = jnp.where(far == 0, second, first)
    pair = jnp.concatenate([col_lo, col_hi], axis=1)
    gathered = lax.all_to_all(jnp.tile(pair, (inner_n, 1)), "inner", 0, 0, tiled=True)
    rows_of_feats = gathered.reshape(length, rows_here)
    weight_rows = in_weight.reshape(rows_here, branches, seq_n, sub).transpose(0, 2, 1, 3)
    partial = jnp.einsum(
        "dgjc,td->gjct", weight_rows, rows_of_feats, preferred_element_type=jnp.float32
    )
    summed = lax.psum_scatter(
        partial.reshape(seq_n, branches * sub, length), "seq", scatter_dimension=0, tiled=True
    )
    summed = summed.reshape(branches, sub, length)
    projected = lax.reduce_precision(summed, exponent_bits=8, mantissa_bits=7)

    taps = lax.dynamic_slice_in_dim(short_taps, place * sub, sub, axis=2)
    decay = lax.dynamic_slice_in_dim(decay_rates, place * sub, sub, axis=1)
    resid = lax.dynamic_slice_in_dim(residues, place * sub, sub, axis=1)
    skip = lax.dynamic_slice_in_dim(skip_gain, place * sub, sub, axis=0)

    rim_rows = taps_count - 1
    extended = jnp.concatenate(
        [jnp.zeros((branches, sub, rim_rows), jnp.float32), projected], axis=2
    )
    short = jnp.zeros((branches, sub, length), jnp.float32)
    for offset_lag in range(taps_count):
        short = (
            short
            + taps[:, offset_lag, :][:, :, None]
            * extended[:, :, rim_rows - offset_lag : rim_rows - offset_lag + length]
        )
    product = short[1] * short[2]
    blocks = length // block_len
    pieces = product.reshape(sub, blocks, block_len)
    amplitude = resid * jnp.sqrt(2.0 * decay)
    offsets = jnp.arange(block_len).astype(jnp.float32)
    falloff = jnp.exp(-decay[:, :, None] * offsets[None, None, :])
    kernel = jnp.einsum("mc,mct->ct", amplitude, falloff, precision=precise)
    lag_grid = jnp.arange(block_len)[:, None] - jnp.arange(block_len)[None, :]
    select = (lag_grid[:, :, None] == jnp.arange(block_len)[None, None, :]).astype(jnp.float32)
    toeplitz = jnp.einsum("tsk,ck->cts", select, kernel, precision=precise)
    inner = jnp.einsum("cts,cbs->cbt", toeplitz, pieces, precision=precise)
    toward_end = jnp.exp(-decay[:, :, None] * (block_len - offsets)[None, None, :])
    block_sums = jnp.einsum("mcs,cbs->mcb", toward_end, pieces, precision=precise)
    later = jnp.arange(blocks)[:, None]
    earlier = jnp.arange(blocks)[None, :]
    distance = jnp.maximum(later - 1 - earlier, 0).astype(jnp.float32)
    carry = jnp.where(
        (earlier < later)[None, None],
        jnp.exp(-decay[:, :, None, None] * (block_len * distance)[None, None]),
        0.0,
    )
    starts = jnp.sum(carry * block_sums[:, :, None, :], axis=3)
    outer = jnp.einsum("mct,mcb->cbt", amplitude[:, :, None] * falloff, starts, precision=precise)
    conv = (inner + outer).reshape(sub, length)
    gated = (short[0] * (conv + skip[:, None] * product)).astype(jnp.bfloat16).T
    outgoing = jnp.broadcast_to(
        gated.reshape(seq_n, 1, tok_rows, sub), (seq_n, outer_n, tok_rows, sub)
    ).reshape(seq_n * outer_n * tok_rows, sub)
    incoming = lax.all_to_all(outgoing, ("seq", "zhi"), 0, 0, tiled=True)
    pair = incoming.reshape(seq_n, outer_n, tok_rows, sub).transpose(2, 1, 0, 3)
    pair = pair.reshape(tok_rows, outer_n * seq_n * sub)
    whole = lax.all_gather(pair, "inner", axis=1, tiled=True)
    weight_out = (
        out_weight.reshape(outer_n, inner_n, channels, -1)
        .transpose(1, 0, 2, 3)
        .reshape(ten_n * channels, -1)
    )
    mixed = jnp.dot(whole, weight_out, preferred_element_type=jnp.float32)
    return mixed.astype(jnp.bfloat16)


def solution(mesh):
    devices = mesh.devices
    halves_mesh = jax.sharding.Mesh(
        devices.reshape(devices.shape[0], devices.shape[1], 2, devices.shape[2] // 2),
        ("dp", "seq", "zhi", "inner"),
    )
    tensor = ("zhi", "inner")
    in_specs = (
        P(("dp", "seq"), tensor),
        P("seq", None, tensor),
        P(None, None, tensor),
        P(None, tensor),
        P(None, tensor),
        P(tensor),
        P(None, tensor),
    )
    out_specs = P(("dp", "seq"), tensor)
    return jax.shard_map(
        body, mesh=halves_mesh, in_specs=in_specs, out_specs=out_specs, check_vma=False
    )
```

```python
import jax
import jax.numpy as jnp
from jax import lax
from jax.sharding import PartitionSpec as P

precise = lax.Precision.HIGHEST
block_len = 64


def body(features, in_weight, short_taps, decay_rates, residues, skip_gain, out_weight):
    seq_n = lax.axis_size("seq")
    outer_n = lax.axis_size("zhi")
    inner_n = lax.axis_size("inner")
    ten_n = outer_n * inner_n
    place = lax.axis_index("seq")
    far = lax.axis_index("zhi")
    lane = far * inner_n + lax.axis_index("inner")
    tok_rows, fcols = features.shape
    rows_here, branches, channels = in_weight.shape
    halves = rows_here // fcols
    sub = channels // seq_n
    length = tok_rows * seq_n
    taps_count = short_taps.shape[1]
    routes = [[], []]
    for s in range(seq_n):
        for c in range(seq_n):
            for e in range(halves):
                for h in range(outer_n):
                    src_id = s * ten_n + c * halves + e
                    dst_id = c * ten_n + h * inner_n + s
                    routes[(e + h) % 2].append((src_id, dst_id))
    first = lax.ppermute(features, ("seq", "zhi", "inner"), routes[0])
    second = lax.ppermute(features, ("seq", "zhi", "inner"), routes[1])
    col_lo = jnp.where(far == 0, first, second)
    col_hi = jnp.where(far == 0, second, first)
    pair = jnp.concatenate([col_lo, col_hi], axis=1)
    gathered = lax.all_to_all(jnp.tile(pair, (inner_n, 1)), "inner", 0, 0, tiled=True)
    rows_of_feats = gathered.reshape(length, rows_here)
    weight_rows = in_weight.reshape(rows_here, branches, seq_n, sub).transpose(0, 2, 1, 3)
    partial = jnp.einsum(
        "dgjc,td->gjct", weight_rows, rows_of_feats, preferred_element_type=jnp.float32
    )
    summed = lax.psum_scatter(
        partial.reshape(seq_n, branches * sub, length), "seq", scatter_dimension=0, tiled=True
    )
    summed = summed.reshape(branches, sub, length)
    projected = lax.reduce_precision(summed, exponent_bits=8, mantissa_bits=7)

    taps = lax.dynamic_slice_in_dim(short_taps, place * sub, sub, axis=2)
    decay = lax.dynamic_slice_in_dim(decay_rates, place * sub, sub, axis=1)
    resid = lax.dynamic_slice_in_dim(residues, place * sub, sub, axis=1)
    skip = lax.dynamic_slice_in_dim(skip_gain, place * sub, sub, axis=0)

    rim_rows = taps_count - 1
    extended = jnp.concatenate(
        [jnp.zeros((branches, sub, rim_rows), jnp.float32), projected], axis=2
    )
    short = jnp.zeros((branches, sub, length), jnp.float32)
    for offset_lag in range(taps_count):
        short = (
            short
            + taps[:, offset_lag, :][:, :, None]
            * extended[:, :, rim_rows - offset_lag : rim_rows - offset_lag + length]
        )
    product = short[1] * short[2]
    blocks = length // block_len
    pieces = product.reshape(sub, blocks, block_len)
    amplitude = resid * jnp.sqrt(2.0 * decay)
    offsets = jnp.arange(block_len).astype(jnp.float32)
    falloff = jnp.exp(-decay[:, :, None] * offsets[None, None, :])
    kernel = jnp.einsum("mc,mct->ct", amplitude, falloff, precision=precise)
    lag_grid = jnp.arange(block_len)[:, None] - jnp.arange(block_len)[None, :]
    select = (lag_grid[:, :, None] == jnp.arange(block_len)[None, None, :]).astype(jnp.float32)
    toeplitz = jnp.einsum("tsk,ck->cts", select, kernel, precision=precise)
    inner = jnp.einsum("cts,cbs->cbt", toeplitz, pieces, precision=precise)
    toward_end = jnp.exp(-decay[:, :, None] * (block_len - offsets)[None, None, :])
    block_sums = jnp.einsum("mcs,cbs->mcb", toward_end, pieces, precision=precise)
    later = jnp.arange(blocks)[:, None]
    earlier = jnp.arange(blocks)[None, :]
    distance = jnp.maximum(later - 1 - earlier, 0).astype(jnp.float32)
    carry = jnp.where(
        (earlier < later)[None, None],
        jnp.exp(-decay[:, :, None, None] * (block_len * distance)[None, None]),
        0.0,
    )
    starts = jnp.sum(carry * block_sums[:, :, None, :], axis=3)
    outer = jnp.einsum("mct,mcb->cbt", amplitude[:, :, None] * falloff, starts, precision=precise)
    conv = (inner + outer).reshape(sub, length)
    gated = (short[0] * (conv + skip[:, None] * product)).astype(jnp.bfloat16).T
    outgoing = jnp.broadcast_to(
        gated.reshape(seq_n, 1, tok_rows, sub), (seq_n, outer_n, tok_rows, sub)
    ).reshape(seq_n * outer_n * tok_rows, sub)
    incoming = lax.all_to_all(outgoing, ("seq", "zhi"), 0, 0, tiled=True)
    pair = incoming.reshape(seq_n, outer_n, tok_rows, sub).transpose(2, 1, 0, 3)
    pair = pair.reshape(tok_rows, outer_n * seq_n * sub)
    whole = lax.all_to_all(jnp.tile(pair, (inner_n, 1)), "inner", 0, 1, tiled=True)
    weight_out = (
        out_weight.reshape(outer_n, inner_n, channels, -1)
        .transpose(1, 0, 2, 3)
        .reshape(ten_n * channels, -1)
    )
    mixed = jnp.dot(whole, weight_out, preferred_element_type=jnp.float32)
    return mixed.astype(jnp.bfloat16)


def solution(mesh):
    devices = mesh.devices
    halves_mesh = jax.sharding.Mesh(
        devices.reshape(devices.shape[0], devices.shape[1], 2, devices.shape[2] // 2),
        ("dp", "seq", "zhi", "inner"),
    )
    tensor = ("zhi", "inner")
    in_specs = (
        P(("dp", "seq"), tensor),
        P("seq", None, tensor),
        P(None, None, tensor),
        P(None, tensor),
        P(None, tensor),
        P(tensor),
        P(None, tensor),
    )
    out_specs = P(("dp", "seq"), tensor)
    return jax.shard_map(
        body, mesh=halves_mesh, in_specs=in_specs, out_specs=out_specs, check_vma=False
    )
```

```python
import jax
import jax.numpy as jnp
from jax import lax
from jax.sharding import PartitionSpec as P

precise = lax.Precision.HIGHEST
block_len = 64


def body(features, in_weight, short_taps, decay_rates, residues, skip_gain, out_weight):
    seq_n = lax.axis_size("seq")
    outer_n = lax.axis_size("zhi")
    inner_n = lax.axis_size("inner")
    ten_n = outer_n * inner_n
    place = lax.axis_index("seq")
    far = lax.axis_index("zhi")
    lane = far * inner_n + lax.axis_index("inner")
    tok_rows, fcols = features.shape
    rows_here, branches, channels = in_weight.shape
    halves = rows_here // fcols
    sub = channels // seq_n
    length = tok_rows * seq_n
    taps_count = short_taps.shape[1]
    routes = [[], []]
    for s in range(seq_n):
        for c in range(seq_n):
            for e in range(halves):
                for h in range(outer_n):
                    src_id = s * ten_n + c * halves + e
                    dst_id = c * ten_n + h * inner_n + s
                    routes[(e + h) % 2].append((src_id, dst_id))
    first = lax.ppermute(features, ("seq", "zhi", "inner"), routes[0])
    second = lax.ppermute(features, ("seq", "zhi", "inner"), routes[1])
    col_lo = jnp.where(far == 0, first, second)
    col_hi = jnp.where(far == 0, second, first)
    pair = jnp.concatenate([col_lo, col_hi], axis=1)
    gathered = lax.all_to_all(jnp.tile(pair, (inner_n, 1)), "inner", 0, 0, tiled=True)
    rows_of_feats = gathered.reshape(length, rows_here)
    weight_rows = in_weight.reshape(rows_here, branches, seq_n, sub).transpose(0, 2, 1, 3)
    partial = jnp.einsum(
        "dgjc,td->gjct", weight_rows, rows_of_feats, preferred_element_type=jnp.float32
    )
    summed = lax.psum_scatter(
        partial.reshape(seq_n, branches * sub, length), "seq", scatter_dimension=0, tiled=True
    )
    summed = summed.reshape(branches, sub, length)
    projected = summed

    taps = lax.dynamic_slice_in_dim(short_taps, place * sub, sub, axis=2)
    decay = lax.dynamic_slice_in_dim(decay_rates, place * sub, sub, axis=1)
    resid = lax.dynamic_slice_in_dim(residues, place * sub, sub, axis=1)
    skip = lax.dynamic_slice_in_dim(skip_gain, place * sub, sub, axis=0)

    rim_rows = taps_count - 1
    extended = lax.reduce_precision(
        jnp.concatenate([jnp.zeros((branches, sub, rim_rows), jnp.float32), projected], axis=2),
        exponent_bits=8,
        mantissa_bits=7,
    )
    short = jnp.zeros((branches, sub, length), jnp.float32)
    for offset_lag in range(taps_count):
        short = (
            short
            + taps[:, offset_lag, :][:, :, None]
            * extended[:, :, rim_rows - offset_lag : rim_rows - offset_lag + length]
        )
    product = short[1] * short[2]
    blocks = length // block_len
    pieces = product.reshape(sub, blocks, block_len)
    amplitude = resid * jnp.sqrt(2.0 * decay)
    offsets = jnp.arange(block_len).astype(jnp.float32)
    falloff = jnp.exp(-decay[:, :, None] * offsets[None, None, :])
    kernel = jnp.einsum("mc,mct->ct", amplitude, falloff, precision=precise)
    lag_grid = jnp.arange(block_len)[:, None] - jnp.arange(block_len)[None, :]
    select = (lag_grid[:, :, None] == jnp.arange(block_len)[None, None, :]).astype(jnp.float32)
    toeplitz = jnp.einsum("tsk,ck->cts", select, kernel, precision=precise)
    inner = jnp.einsum("cts,cbs->cbt", toeplitz, pieces, precision=precise)
    toward_end = jnp.exp(-decay[:, :, None] * (block_len - offsets)[None, None, :])
    block_sums = jnp.einsum("mcs,cbs->mcb", toward_end, pieces, precision=precise)
    later = jnp.arange(blocks)[:, None]
    earlier = jnp.arange(blocks)[None, :]
    distance = jnp.maximum(later - 1 - earlier, 0).astype(jnp.float32)
    carry = jnp.where(
        (earlier < later)[None, None],
        jnp.exp(-decay[:, :, None, None] * (block_len * distance)[None, None]),
        0.0,
    )
    starts = jnp.sum(carry * block_sums[:, :, None, :], axis=3)
    outer = jnp.einsum("mct,mcb->cbt", amplitude[:, :, None] * falloff, starts, precision=precise)
    conv = (inner + outer).reshape(sub, length)
    gated = (short[0] * (conv + skip[:, None] * product)).astype(jnp.bfloat16).T
    outgoing = jnp.broadcast_to(
        gated.reshape(seq_n, 1, tok_rows, sub), (seq_n, outer_n, tok_rows, sub)
    ).reshape(seq_n * outer_n * tok_rows, sub)
    incoming = lax.all_to_all(outgoing, ("seq", "zhi"), 0, 0, tiled=True)
    pair = incoming.reshape(seq_n, outer_n, tok_rows, sub).transpose(2, 1, 0, 3)
    pair = pair.reshape(tok_rows, outer_n * seq_n * sub)
    whole = lax.all_to_all(jnp.tile(pair, (inner_n, 1)), "inner", 0, 1, tiled=True)
    weight_out = (
        out_weight.reshape(outer_n, inner_n, channels, -1)
        .transpose(1, 0, 2, 3)
        .reshape(ten_n * channels, -1)
    )
    mixed = jnp.dot(whole, weight_out, preferred_element_type=jnp.float32)
    return mixed.astype(jnp.bfloat16)


def solution(mesh):
    devices = mesh.devices
    halves_mesh = jax.sharding.Mesh(
        devices.reshape(devices.shape[0], devices.shape[1], 2, devices.shape[2] // 2),
        ("dp", "seq", "zhi", "inner"),
    )
    tensor = ("zhi", "inner")
    in_specs = (
        P(("dp", "seq"), tensor),
        P("seq", None, tensor),
        P(None, None, tensor),
        P(None, tensor),
        P(None, tensor),
        P(tensor),
        P(None, tensor),
    )
    out_specs = P(("dp", "seq"), tensor)
    return jax.shard_map(
        body, mesh=halves_mesh, in_specs=in_specs, out_specs=out_specs, check_vma=False
    )
```
